512 devices in a mesh: ctx: 64 (over y, x, core), head: 8 (over z).
Axes of the slice: x: 4, y: 8, z: 8, core: 2. Of those that a mesh axis runs over, the one named last changes fastest.
Arguments:
- tokens: bfloat16 [65536, 2048], P('ctx', 'head'), may hold values from -6 to 6
- w_qkv: bfloat16 [3, 2048, 2048], P(None, 'ctx', 'head'), may hold values from -0.125 to 0.125
- out_gain: float32 [2048], P('head'), may hold values from 0.25 to 1.75
- seg_ids: int32 [65536], P('ctx'), may hold values from 0 to 15, never falling along the last dimension, each value on 1 to 16384 neighbouring positions
Outputs:
- attended: bfloat16 [65536, 2048], P('ctx', 'head')
The draws below stay inside these ranges and needn't reach their ends.
Inputs may be any that keep to these rules, and one draw needn't show every extreme that they name: `seg_ids`: segment numbers never fall along the stream; each segment covers 1 to 16384 consecutive tokens, and one covers exactly 16384.
All inputs are finite; a program needn't handle non-finite values.
Results may differ from the reference program's by a relative error of at most 0.012.
Values may be sent and summed in bfloat16 or wider, within the bound.
No kernel may reach another device: no remote copies, remote signals or barrier semaphores. Data moves between devices by JAX's collectives and lax.ppermute only.
A program may use at most 64 MiB of HBM per device.

```python
import math
import jax
import jax.numpy as jnp
import numpy as np
from jax import lax

HEADS = 16
HEAD_DIM = 128
D = 2048
TOK_DEV = 1024
TOKENS = 65536
SEGS = 16
SPAN = 16384
N_CTX = 64


def block_levels(stream_key, extent, shards, least, largest):
    def one(position, parts):
        draws = jax.random.uniform(jax.random.fold_in(jax.random.fold_in(stream_key, 6), position), (parts,), jnp.float32, least / len(shards), largest / len(shards))
        return jnp.repeat(jnp.exp(draws), extent[position] // parts).reshape((-1,) + (1,) * (len(extent) - position - 1))

    loudness = one(*shards[0])
    for cut in shards[1:]:
        loudness = loudness * one(*cut)
    return loudness


def split_up(number_of, total, bound, lean):
    loads = [(1 << 20) // math.isqrt(standing ** lean) + 1 for standing in range(2, number_of + 1)]
    spare, holding = total - bound - (number_of - 1), [1] * (number_of - 1)
    while spare > 0:
        movable = [i for i in range(number_of - 1) if holding[i] < bound]
        pool, budget = sum([loads[i] for i in movable]), spare
        for i in movable:
            extra = min(bound - holding[i], max(1, budget * loads[i] // pool), spare)
            holding[i] = holding[i] + extra
            spare = spare - extra
    return np.array([bound] + holding)


def ragged_sizes(key, count, total, most, lean):
    if count == 2:
        one = jax.random.randint(key, (), max(1, total - most), min(most, total - 1) + 1)
        return jnp.stack([one, total - one])
    tallies = jnp.asarray(split_up(count, total, most, lean), jnp.int32)
    twos = (count - 1) // 2
    donor, sink = tallies[1:1 + 2 * twos:2], tallies[2:2 + 2 * twos:2]
    slack = jnp.minimum(donor - 1, most - sink)
    passed = jax.random.randint(jax.random.fold_in(key, 1), (twos,), 0, 1 << 20) % (slack + 1)
    tallies = tallies.at[1:1 + 2 * twos:2].set(donor - passed).at[2:2 + 2 * twos:2].set(sink + passed)
    return tallies[jax.random.permutation(jax.random.fold_in(key, 2), count)]


def noise(own_key, dims, deviation, limit, shards=(), held_as=jnp.bfloat16):
    entries = jax.random.normal(own_key, dims, jnp.float32) * deviation
    if len(shards) > 0:
        entries = block_levels(own_key, dims, shards, -0.22, 0.18) * entries
    return jnp.clip(entries, min=-limit, max=limit).astype(held_as)


def setup_inputs(seed: int = 0) -> dict:
    seeds = jax.random.split(jax.random.key(seed), 5)
    return {
        "tokens": noise(seeds[0], (TOKENS, D), 1.0, 6.0, ((0, 64), (1, 8))),
        "w_qkv": noise(seeds[1], (3, D, D), D ** -0.5, 0.125, ((1, 64), (2, 8))),
        "out_gain": jnp.clip(1.0 + 0.15 * jax.random.normal(seeds[2], (D,), jnp.float32), 0.25, 1.75),
        "seg_ids": jnp.searchsorted(jnp.cumsum(ragged_sizes(seeds[3], SEGS, TOKENS, SPAN, 2)), jnp.arange(TOKENS), side="right").astype(jnp.int32),
    }


def feature_map(values):
    return (jax.nn.elu(values.astype(jnp.float32)) + 1.0).astype(jnp.bfloat16)

def combine(earlier, later):
    first_state, first_tail = earlier
    later_state, later_tail = later
    linked = (first_tail == later_tail) | (later_tail < 0.0)
    return (later_state + jnp.where(linked, first_state, 0.0), jnp.where(later_tail < 0.0, first_tail, later_tail))

def prepare(projected, segment):
    row_count = segment.shape[0]
    head_count = projected.shape[2] // HEAD_DIM
    queries = feature_map(projected[0]).reshape(row_count, head_count, HEAD_DIM)
    key_map = feature_map(projected[1]).reshape(row_count, head_count, HEAD_DIM)
    values = projected[2].reshape(row_count, head_count, HEAD_DIM)
    seg_float = segment.astype(jnp.float32)
    tail_id = seg_float[-1]
    key_tail = jnp.where((seg_float == tail_id)[:, None, None], key_map, jnp.zeros_like(key_map))
    kv_state = jnp.einsum('thd,the->hde', key_tail.astype(jnp.float32), values.astype(jnp.float32))
    return (queries, key_map, values, seg_float, kv_state, tail_id)

def complete(queries, key_map, values, seg_float, state_in, tail_in, out_gain):
    row_count, head_count = (queries.shape[0], queries.shape[1])
    state_low = state_in.astype(jnp.bfloat16)
    prefix = jnp.einsum('thd,hde->the', queries.astype(jnp.float32), state_low.astype(jnp.float32))
    prefix = jnp.where((seg_float == tail_in)[:, None, None], prefix, 0.0)
    block_rows = min(512, row_count)
    positions = jnp.arange(row_count, dtype=jnp.int32)

    def one_block(blk_no):
        first_row = (blk_no * block_rows).astype(jnp.int32)
        query_blk = lax.dynamic_slice_in_dim(queries, first_row, block_rows, 0)
        query_pos = first_row + jnp.arange(block_rows, dtype=jnp.int32)
        query_seg = lax.dynamic_slice_in_dim(seg_float, first_row, block_rows, 0)
        scores = jnp.einsum('bhd,shd->hbs', query_blk.astype(jnp.float32), key_map.astype(jnp.float32))
        visible = (positions[None, :] <= query_pos[:, None]) & (seg_float[None, :] == query_seg[:, None])
        weights = jnp.where(visible[None], scores, 0.0).astype(jnp.bfloat16)
        return jnp.einsum('hbs,she->bhe', weights.astype(jnp.float32), values.astype(jnp.float32))
    local_part = lax.map(one_block, jnp.arange(row_count // block_rows, dtype=jnp.int32))
    numerator = local_part.reshape(row_count, head_count, HEAD_DIM) + prefix
    inv_norm = lax.rsqrt(lax.optimization_barrier(jnp.mean(numerator * numerator, axis=-1, keepdims=True)) + 1e-05)
    result = numerator * inv_norm * out_gain.reshape(head_count, HEAD_DIM)
    return result.astype(jnp.bfloat16).reshape(row_count, head_count * HEAD_DIM)

def reference(tokens, w_qkv, out_gain, seg_ids):
    blocks = tokens.reshape(N_CTX, TOK_DEV, D)
    segments = seg_ids.reshape(N_CTX, TOK_DEV)
    weights_wide = w_qkv.astype(jnp.float32)

    def one_step(carried, item):
        block_tok, segment = item
        projected = jnp.einsum('td,gde->gte', block_tok.astype(jnp.float32), weights_wide).astype(jnp.bfloat16)
        queries, key_map, values, seg_float, kv_state, tail_id = prepare(projected, segment)
        result = complete(queries, key_map, values, seg_float, carried[0], carried[1], out_gain)
        return (combine(carried, (kv_state, tail_id)), result)
    initial = (jnp.zeros((HEADS, HEAD_DIM, HEAD_DIM), jnp.float32), jnp.array(-1.0, jnp.float32))
    _, results = lax.scan(one_step, initial, (blocks, segments))
    return results.reshape(TOKENS, D)
```

```python
import jax
import jax.numpy as jnp
from jax import lax
from jax.sharding import PartitionSpec as P

HEAD_DIM = 128
SPAN = 16384


def shifted(value, axis, steps):
    count = lax.axis_size(axis)
    return lax.ppermute(value, axis, [(source, source + steps) for source in range(count - steps)])


def feature_map(values):
    return (jax.nn.elu(values.astype(jnp.float32)) + 1.0).astype(jnp.bfloat16)


def state_scan(kv_state, tail_id, row_count):
    head_count = kv_state.shape[0]
    flat = kv_state.reshape(head_count * HEAD_DIM, HEAD_DIM)
    tail_rows = jnp.full((8, HEAD_DIM), tail_id, jnp.float32)
    packed = jnp.concatenate([flat, tail_rows], axis=0)
    state_rows = head_count * HEAD_DIM
    is_state = (jnp.arange(packed.shape[0]) < state_rows)[:, None]
    count = lax.axis_size("ctx")
    window = min(count - 1, 1 + (SPAN - 1) // row_count)
    running = shifted(packed, "ctx", 1)
    step = 1
    while step < window:
        incoming = shifted(running, "ctx", step)
        linked = incoming[state_rows, 0] == running[state_rows, 0]
        running = running + jnp.where(is_state & linked, incoming, 0.0)
        step *= 2
    state_in = running[:state_rows].reshape(head_count, HEAD_DIM, HEAD_DIM)
    return state_in, running[state_rows, 0]


def per_device(tokens, w_qkv, out_gain, seg_ids):
    whole = lax.all_gather(tokens, "head", axis=1, tiled=True)
    projected = jnp.einsum(
        "tr,grc->gtc",
        whole,
        lax.all_gather(w_qkv, "ctx", axis=1, tiled=True),
        preferred_element_type=jnp.float32,
    ).astype(jnp.bfloat16)
    row_count = seg_ids.shape[0]
    head_count = projected.shape[2] // HEAD_DIM
    queries = feature_map(projected[0]).reshape(row_count, head_count, HEAD_DIM)
    key_map = feature_map(projected[1]).reshape(row_count, head_count, HEAD_DIM)
    values = projected[2].reshape(row_count, head_count, HEAD_DIM)
    seg_float = seg_ids.astype(jnp.float32)
    tail_id = seg_float[-1]
    key_tail = jnp.where((seg_float == tail_id)[:, None, None], key_map, jnp.zeros_like(key_map))
    kv_state = jnp.einsum("thd,the->hde", key_tail, values, preferred_element_type=jnp.float32)

    state_in, tail_in = state_scan(kv_state, tail_id, row_count)

    block_rows = min(512, row_count)
    pieces = []
    for blk_no in range(row_count // block_rows):
        first_row = blk_no * block_rows
        key_end = first_row + block_rows
        query_blk = queries[first_row:key_end]
        query_pos = first_row + jnp.arange(block_rows, dtype=jnp.int32)
        query_seg = seg_float[first_row:key_end]
        scores = jnp.einsum(
            "bhd,shd->hbs", query_blk, key_map[:key_end], preferred_element_type=jnp.float32
        )
        visible = (jnp.arange(key_end, dtype=jnp.int32)[None, :] <= query_pos[:, None]) & (
            seg_float[None, :key_end] == query_seg[:, None]
        )
        weights = jnp.where(visible[None], scores, 0.0).astype(jnp.bfloat16)
        pieces.append(
            jnp.einsum("hbs,she->bhe", weights, values[:key_end], preferred_element_type=jnp.float32)
        )
    local_part = jnp.concatenate(pieces, axis=0)

    state_low = state_in.astype(jnp.bfloat16)
    prefix = jnp.einsum("thd,hde->the", queries, state_low, preferred_element_type=jnp.float32)
    prefix = jnp.where((seg_float == tail_in)[:, None, None], prefix, 0.0)
    numerator = local_part + prefix
    inv_norm = lax.rsqrt(jnp.mean(numerator * numerator, axis=-1, keepdims=True) + 1e-05)
    result = numerator * inv_norm * out_gain.reshape(head_count, HEAD_DIM)
    return result.astype(jnp.bfloat16).reshape(row_count, head_count * HEAD_DIM)


def solution(mesh):
    placed = (P("ctx", "head"), P(None, "ctx", "head"), P("head"), P("ctx"))
    return jax.shard_map(
        per_device, mesh=mesh, in_specs=placed, out_specs=P("ctx", "head"), check_vma=False
    )
```

```python
import jax
import jax.numpy as jnp
from jax import lax
from jax.sharding import Mesh
from jax.sharding import PartitionSpec as P

HEAD_DIM = 128
SPAN = 16384


CTX = ("y", "x", "core")


def shifted(value, axis, steps, count):
    return lax.ppermute(value, axis, [(source, source + steps) for source in range(count - steps)])


def ring_gather(value, axis, count, dim):
    by_offset = {0: value}
    ahead = value
    behind = value
    for step in range(1, count // 2 + 1):
        ahead = lax.ppermute(ahead, axis, [(j, (j + 1) % count) for j in range(count)])
        by_offset[-step] = ahead
        if step < count - count // 2:
            behind = lax.ppermute(behind, axis, [(j, (j - 1) % count) for j in range(count)])
            by_offset[step] = behind
    low = -(count // 2)
    stacked = jnp.stack([by_offset[off] for off in range(low, low + count)], axis=0)
    ordered = jnp.roll(stacked, lax.axis_index(axis) + low, axis=0)
    moved = jnp.moveaxis(ordered, 0, dim)
    shape = list(value.shape)
    shape[dim] *= count
    return moved.reshape(shape)


def feature_map(values):
    return (jax.nn.elu(values.astype(jnp.float32)) + 1.0).astype(jnp.bfloat16)


def state_scan(kv_state, tail_id, row_count):
    head_count = kv_state.shape[0]
    flat = kv_state.reshape(head_count * HEAD_DIM, HEAD_DIM)
    tail_rows = jnp.full((8, HEAD_DIM), tail_id, jnp.float32)
    packed = jnp.concatenate([flat, tail_rows], axis=0)
    state_rows = head_count * HEAD_DIM
    is_state = (jnp.arange(packed.shape[0]) < state_rows)[:, None]
    count = lax.axis_size(CTX)
    window = min(count - 1, 1 + (SPAN - 1) // row_count)
    running = shifted(packed, CTX, 1, count)
    step = 1
    while step < window:
        incoming = shifted(running, CTX, step, count)
        linked = incoming[state_rows, 0] == running[state_rows, 0]
        running = running + jnp.where(is_state & linked, incoming, 0.0)
        step *= 2
    state_in = running[:state_rows].reshape(head_count, HEAD_DIM, HEAD_DIM)
    return state_in, running[state_rows, 0]


def per_device(tokens, w_qkv, out_gain, seg_ids):
    whole = lax.all_gather(tokens, "head", axis=1, tiled=True)
    w_rows = lax.all_gather(w_qkv, "core", axis=1, tiled=True)
    w_rows = ring_gather(w_rows, "x", lax.axis_size("x"), 1)
    w_rows = ring_gather(w_rows, "y", lax.axis_size("y"), 1)
    projected = jnp.einsum(
        "tr,grc->gtc", whole, w_rows, preferred_element_type=jnp.float32
    ).astype(jnp.bfloat16)
    row_count = seg_ids.shape[0]
    head_count = projected.shape[2] // HEAD_DIM
    queries = feature_map(projected[0]).reshape(row_count, head_count, HEAD_DIM)
    key_map = feature_map(projected[1]).reshape(row_count, head_count, HEAD_DIM)
    values = projected[2].reshape(row_count, head_count, HEAD_DIM)
    seg_float = seg_ids.astype(jnp.float32)
    tail_id = seg_float[-1]
    key_tail = jnp.where((seg_float == tail_id)[:, None, None], key_map, jnp.zeros_like(key_map))
    kv_state = jnp.einsum("thd,the->hde", key_tail, values, preferred_element_type=jnp.float32)

    state_in, tail_in = state_scan(kv_state, tail_id, row_count)

    block_rows = min(512, row_count)
    pieces = []
    for blk_no in range(row_count // block_rows):
        first_row = blk_no * block_rows
        key_end = first_row + block_rows
        query_blk = queries[first_row:key_end]
        query_pos = first_row + jnp.arange(block_rows, dtype=jnp.int32)
        query_seg = seg_float[first_row:key_end]
        scores = jnp.einsum(
            "bhd,shd->hbs", query_blk, key_map[:key_end], preferred_element_type=jnp.float32
        )
        visible = (jnp.arange(key_end, dtype=jnp.int32)[None, :] <= query_pos[:, None]) & (
            seg_float[None, :key_end] == query_seg[:, None]
        )
        weights = jnp.where(visible[None], scores, 0.0).astype(jnp.bfloat16)
        pieces.append(
            jnp.einsum("hbs,she->bhe", weights, values[:key_end], preferred_element_type=jnp.float32)
        )
    local_part = jnp.concatenate(pieces, axis=0)

    state_low = state_in.astype(jnp.bfloat16)
    prefix = jnp.einsum("thd,hde->the", queries, state_low, preferred_element_type=jnp.float32)
    prefix = jnp.where((seg_float == tail_in)[:, None, None], prefix, 0.0)
    numerator = local_part + prefix
    inv_norm = lax.rsqrt(jnp.mean(numerator * numerator, axis=-1, keepdims=True) + 1e-05)
    result = numerator * inv_norm * out_gain.reshape(head_count, HEAD_DIM)
    return result.astype(jnp.bfloat16).reshape(row_count, head_count * HEAD_DIM)


def solution(mesh):
    shape = dict(zip(mesh.axis_names, mesh.devices.shape))
    head = shape["head"]
    fine = Mesh(mesh.devices.reshape(-1, 4, 2, head), (*CTX, "head"))
    placed = (P(CTX, "head"), P(None, CTX, "head"), P("head"), P(CTX))
    return jax.shard_map(
        per_device, mesh=fine, in_specs=placed, out_specs=P(CTX, "head"), check_vma=False
    )
```

```python
import jax
import jax.numpy as jnp
from jax import lax
from jax.sharding import Mesh
from jax.sharding import PartitionSpec as P

HEAD_DIM = 128
SPAN = 16384


CTX = ("y", "x", "core")


def shifted(value, axis, steps, count):
    return lax.ppermute(value, axis, [(source, source + steps) for source in range(count - steps)])


def ring_gather(value, axis, count, dim):
    by_offset = {0: value}
    ahead = value
    behind = value
    for step in range(1, count // 2 + 1):
        ahead = lax.ppermute(ahead, axis, [(j, (j + 1) % count) for j in range(count)])
        by_offset[-step] = ahead
        if step < count - count // 2:
            behind = lax.ppermute(behind, axis, [(j, (j - 1) % count) for j in range(count)])
            by_offset[step] = behind
    low = -(count // 2)
    stacked = jnp.stack([by_offset[off] for off in range(low, low + count)], axis=0)
    ordered = jnp.roll(stacked, lax.axis_index(axis) + low, axis=0)
    moved = jnp.moveaxis(ordered, 0, dim)
    shape = list(value.shape)
    shape[dim] *= count
    return moved.reshape(shape)


def gather_weights(w_local):
    half = w_local.shape[2] // 2
    core = lax.axis_index("core")
    partner = lax.ppermute(w_local, "core", [(0, 1), (1, 0)])
    low_rows = jnp.where(core == 0, w_local[:, :, :half], partner[:, :, half:])
    high_rows = jnp.where(core == 0, partner[:, :, :half], w_local[:, :, half:])
    rows = jnp.concatenate([low_rows, high_rows], axis=1)
    rows = ring_gather(rows, "x", lax.axis_size("x"), 1)
    rows = ring_gather(rows, "y", lax.axis_size("y"), 1)
    other = lax.ppermute(rows, "core", [(0, 1), (1, 0)])
    return jnp.where(
        core == 0,
        jnp.concatenate([rows, other], axis=2),
        jnp.concatenate([other, rows], axis=2),
    )


def feature_map(values):
    return (jax.nn.elu(values.astype(jnp.float32)) + 1.0).astype(jnp.bfloat16)


def state_scan(kv_state, tail_id, row_count):
    head_count = kv_state.shape[0]
    flat = kv_state.reshape(head_count * HEAD_DIM, HEAD_DIM)
    tail_rows = jnp.full((8, HEAD_DIM), tail_id, jnp.float32)
    packed = jnp.concatenate([flat, tail_rows], axis=0)
    state_rows = head_count * HEAD_DIM
    is_state = (jnp.arange(packed.shape[0]) < state_rows)[:, None]
    count = lax.axis_size(CTX)
    window = min(count - 1, 1 + (SPAN - 1) // row_count)
    running = shifted(packed, CTX, 1, count)
    step = 1
    while step < window:
        incoming = shifted(running, CTX, step, count)
        linked = incoming[state_rows, 0] == running[state_rows, 0]
        running = running + jnp.where(is_state & linked, incoming, 0.0)
        step *= 2
    state_in = running[:state_rows].reshape(head_count, HEAD_DIM, HEAD_DIM)
    return state_in, running[state_rows, 0]


def per_device(tokens, w_qkv, out_gain, seg_ids):
    whole = lax.all_gather(tokens, "head", axis=1, tiled=True)
    w_rows = gather_weights(w_qkv)
    projected = jnp.einsum(
        "tr,grc->gtc", whole, w_rows, preferred_element_type=jnp.float32
    ).astype(jnp.bfloat16)
    row_count = seg_ids.shape[0]
    head_count = projected.shape[2] // HEAD_DIM
    queries = feature_map(projected[0]).reshape(row_count, head_count, HEAD_DIM)
    key_map = feature_map(projected[1]).reshape(row_count, head_count, HEAD_DIM)
    values = projected[2].reshape(row_count, head_count, HEAD_DIM)
    seg_float = seg_ids.astype(jnp.float32)
    tail_id = seg_float[-1]
    key_tail = jnp.where((seg_float == tail_id)[:, None, None], key_map, jnp.zeros_like(key_map))
    kv_state = jnp.einsum("thd,the->hde", key_tail, values, preferred_element_type=jnp.float32)

    state_in, tail_in = state_scan(kv_state, tail_id, row_count)

    block_rows = min(512, row_count)
    pieces = []
    for blk_no in range(row_count // block_rows):
        first_row = blk_no * block_rows
        key_end = first_row + block_rows
        query_blk = queries[first_row:key_end]
        query_pos = first_row + jnp.arange(block_rows, dtype=jnp.int32)
        query_seg = seg_float[first_row:key_end]
        scores = jnp.einsum(
            "bhd,shd->hbs", query_blk, key_map[:key_end], preferred_element_type=jnp.float32
        )
        visible = (jnp.arange(key_end, dtype=jnp.int32)[None, :] <= query_pos[:, None]) & (
            seg_float[None, :key_end] == query_seg[:, None]
        )
        weights = jnp.where(visible[None], scores, 0.0).astype(jnp.bfloat16)
        pieces.append(
            jnp.einsum("hbs,she->bhe", weights, values[:key_end], preferred_element_type=jnp.float32)
        )
    local_part = jnp.concatenate(pieces, axis=0)

    state_low = state_in.astype(jnp.bfloat16)
    prefix = jnp.einsum("thd,hde->the", queries, state_low, preferred_element_type=jnp.float32)
    prefix = jnp.where((seg_float == tail_in)[:, None, None], prefix, 0.0)
    numerator = local_part + prefix
    inv_norm = lax.rsqrt(jnp.mean(numerator * numerator, axis=-1, keepdims=True) + 1e-05)
    result = numerator * inv_norm * out_gain.reshape(head_count, HEAD_DIM)
    return result.astype(jnp.bfloat16).reshape(row_count, head_count * HEAD_DIM)


def solution(mesh):
    shape = dict(zip(mesh.axis_names, mesh.devices.shape))
    head = shape["head"]
    fine = Mesh(mesh.devices.reshape(-1, 4, 2, head), (*CTX, "head"))
    placed = (P(CTX, "head"), P(None, CTX, "head"), P("head"), P(CTX))
    return jax.shard_map(
        per_device, mesh=fine, in_specs=placed, out_specs=P(CTX, "head"), check_vma=False
    )
```

```python
import jax
import jax.numpy as jnp
from jax import lax
from jax.sharding import Mesh
from jax.sharding import PartitionSpec as P

HEAD_DIM = 128
SPAN = 16384


CTX = ("y", "x", "core")


def shifted(value, axis, steps, count):
    return lax.ppermute(value, axis, [(source, source + steps) for source in range(count - steps)])


def ring_gather(value, axis, count, dim):
    by_offset = {0: value}
    ahead = value
    behind = value
    for step in range(1, count // 2 + 1):
        ahead = lax.ppermute(ahead, axis, [(j, (j + 1) % count) for j in range(count)])
        by_offset[-step] = ahead
        if step < count - count // 2:
            behind = lax.ppermute(behind, axis, [(j, (j - 1) % count) for j in range(count)])
            by_offset[step] = behind
    low = -(count // 2)
    stacked = jnp.stack([by_offset[off] for off in range(low, low + count)], axis=0)
    ordered = jnp.roll(stacked, lax.axis_index(axis) + low, axis=0)
    moved = jnp.moveaxis(ordered, 0, dim)
    shape = list(value.shape)
    shape[dim] *= count
    return moved.reshape(shape)


def gather_weights(w_local):
    half = w_local.shape[2] // 2
    core = lax.axis_index("core")
    partner = lax.ppermute(w_local, "core", [(0, 1), (1, 0)])
    low_rows = jnp.where(core == 0, w_local[:, :, :half], partner[:, :, half:])
    high_rows = jnp.where(core == 0, partner[:, :, :half], w_local[:, :, half:])
    rows = jnp.concatenate([low_rows, high_rows], axis=1)
    rows = ring_gather(rows, "x", lax.axis_size("x"), 1)
    rows = ring_gather(rows, "y", lax.axis_size("y"), 1)
    other = lax.ppermute(rows, "core", [(0, 1), (1, 0)])
    return jnp.where(
        core == 0,
        jnp.concatenate([rows, other], axis=2),
        jnp.concatenate([other, rows], axis=2),
    )


def feature_map(values):
    return (jax.nn.elu(values.astype(jnp.float32)) + 1.0).astype(jnp.bfloat16)


def state_scan(kv_state, tail_id, row_count):
    head_count = kv_state.shape[0]
    state_rows = head_count * HEAD_DIM
    flat = kv_state.reshape(state_rows, HEAD_DIM)
    packed = jnp.concatenate([flat, jnp.full((8, HEAD_DIM), tail_id, jnp.float32)], axis=0)
    row_len = lax.axis_size("x") * lax.axis_size("core")
    window = min(lax.axis_size(CTX) - 1, 1 + (SPAN - 1) // row_count)
    assert window <= 2 * row_len
    row = lax.all_gather(packed, ("x", "core"), axis=0, tiled=False)
    states = row[:, :state_rows]
    tails = row[:, state_rows, 0]
    pos = lax.axis_index("x") * lax.axis_size("core") + lax.axis_index("core")
    places = jnp.arange(row_len)
    last_tail = tails[row_len - 1]
    in_tail = tails == last_tail
    row_total = jnp.sum(jnp.where(in_tail[:, None, None], states, 0.0), axis=0)
    row_rest = jnp.sum(jnp.where((in_tail & (places >= pos))[:, None, None], states, 0.0), axis=0)
    tail_block = jnp.full((8, HEAD_DIM), last_tail, jnp.float32)
    y_count = lax.axis_size("y")
    one_back = shifted(jnp.concatenate([row_total, tail_block], axis=0), "y", 1, y_count)
    two_back = shifted(jnp.concatenate([row_rest, tail_block], axis=0), "y", 2, y_count)
    prev_tail = jnp.where(pos > 0, tails[jnp.maximum(pos - 1, 0)], one_back[state_rows, 0])
    before = (places < pos) & (tails == prev_tail)
    state = jnp.sum(jnp.where(before[:, None, None], states, 0.0), axis=0)
    state = state + jnp.where(one_back[state_rows, 0] == prev_tail, one_back[:state_rows], 0.0)
    if window > row_len:
        state = state + jnp.where(two_back[state_rows, 0] == prev_tail, two_back[:state_rows], 0.0)
    return state.reshape(head_count, HEAD_DIM, HEAD_DIM), prev_tail


def per_device(tokens, w_qkv, out_gain, seg_ids):
    whole = lax.all_gather(tokens, "head", axis=1, tiled=True)
    w_rows = gather_weights(w_qkv)
    projected = jnp.einsum(
        "tr,grc->gtc", whole, w_rows, preferred_element_type=jnp.float32
    ).astype(jnp.bfloat16)
    row_count = seg_ids.shape[0]
    head_count = projected.shape[2] // HEAD_DIM
    queries = feature_map(projected[0]).reshape(row_count, head_count, HEAD_DIM)
    key_map = feature_map(projected[1]).reshape(row_count, head_count, HEAD_DIM)
    values = projected[2].reshape(row_count, head_count, HEAD_DIM)
    seg_float = seg_ids.astype(jnp.float32)
    tail_id = seg_float[-1]
    key_tail = jnp.where((seg_float == tail_id)[:, None, None], key_map, jnp.zeros_like(key_map))
    kv_state = jnp.einsum("thd,the->hde", key_tail, values, preferred_element_type=jnp.float32)

    state_in, tail_in = state_scan(kv_state, tail_id, row_count)

    block_rows = min(512, row_count)
    pieces = []
    for blk_no in range(row_count // block_rows):
        first_row = blk_no * block_rows
        key_end = first_row + block_rows
        query_blk = queries[first_row:key_end]
        query_pos = first_row + jnp.arange(block_rows, dtype=jnp.int32)
        query_seg = seg_float[first_row:key_end]
        scores = jnp.einsum(
            "bhd,shd->hbs", query_blk, key_map[:key_end], preferred_element_type=jnp.float32
        )
        visible = (jnp.arange(key_end, dtype=jnp.int32)[None, :] <= query_pos[:, None]) & (
            seg_float[None, :key_end] == query_seg[:, None]
        )
        weights = jnp.where(visible[None], scores, 0.0).astype(jnp.bfloat16)
        pieces.append(
            jnp.einsum("hbs,she->bhe", weights, values[:key_end], preferred_element_type=jnp.float32)
        )
    local_part = jnp.concatenate(pieces, axis=0)

    state_low = state_in.astype(jnp.bfloat16)
    prefix = jnp.einsum("thd,hde->the", queries, state_low, preferred_element_type=jnp.float32)
    prefix = jnp.where((seg_float == tail_in)[:, None, None], prefix, 0.0)
    numerator = local_part + prefix
    inv_norm = lax.rsqrt(jnp.mean(numerator * numerator, axis=-1, keepdims=True) + 1e-05)
    result = numerator * inv_norm * out_gain.reshape(head_count, HEAD_DIM)
    return result.astype(jnp.bfloat16).reshape(row_count, head_count * HEAD_DIM)


def solution(mesh):
    shape = dict(zip(mesh.axis_names, mesh.devices.shape))
    head = shape["head"]
    fine = Mesh(mesh.devices.reshape(-1, 4, 2, head), (*CTX, "head"))
    placed = (P(CTX, "head"), P(None, CTX, "head"), P("head"), P(CTX))
    return jax.shard_map(
        per_device, mesh=fine, in_specs=placed, out_specs=P(CTX, "head"), check_vma=False
    )
```

```python
import jax
import jax.numpy as jnp
from jax import lax
from jax.sharding import Mesh
from jax.sharding import PartitionSpec as P

HEAD_DIM = 128
SPAN = 16384


CTX = ("y", "x", "core")


def shifted(value, axis, steps, count):
    return lax.ppermute(value, axis, [(source, source + steps) for source in range(count - steps)])


def ring_gather(value, axis, count, dim):
    by_offset = {0: value}
    ahead = value
    behind = value
    for step in range(1, count // 2 + 1):
        ahead = lax.ppermute(ahead, axis, [(j, (j + 1) % count) for j in range(count)])
        by_offset[-step] = ahead
        if step < count - count // 2:
            behind = lax.ppermute(behind, axis, [(j, (j - 1) % count) for j in range(count)])
            by_offset[step] = behind
    low = -(count // 2)
    stacked = jnp.stack([by_offset[off] for off in range(low, low + count)], axis=0)
    ordered = jnp.roll(stacked, lax.axis_index(axis) + low, axis=0)
    moved = jnp.moveaxis(ordered, 0, dim)
    shape = list(value.shape)
    shape[dim] *= count
    return moved.reshape(shape)


def gather_weights(w_local):
    half = w_local.shape[2] // 2
    core = lax.axis_index("core")
    partner = lax.ppermute(w_local, "core", [(0, 1), (1, 0)])
    low_rows = jnp.where(core == 0, w_local[:, :, :half], partner[:, :, half:])
    high_rows = jnp.where(core == 0, partner[:, :, :half], w_local[:, :, half:])
    rows = jnp.concatenate([low_rows, high_rows], axis=1)
    rows = ring_gather(rows, "x", lax.axis_size("x"), 1)
    rows = ring_gather(rows, "y", lax.axis_size("y"), 1)
    other = lax.ppermute(rows, "core", [(0, 1), (1, 0)])
    return jnp.where(
        core == 0,
        jnp.concatenate([rows, other], axis=2),
        jnp.concatenate([other, rows], axis=2),
    )


def feature_map(values):
    return (jax.nn.elu(values.astype(jnp.float32)) + 1.0).astype(jnp.bfloat16)


def state_scan(kv_state, tail_id, row_count):
    head_count = kv_state.shape[0]
    state_rows = head_count * HEAD_DIM
    flat = kv_state.reshape(state_rows, HEAD_DIM)
    count = lax.axis_size(CTX)
    window = min(count - 1, 1 + (SPAN - 1) // row_count)
    packed = jnp.concatenate([flat, jnp.full((8, HEAD_DIM), tail_id, jnp.float32)], axis=0)
    radix = 4
    span = 1
    running = None
    while span < window:
        got = [shifted(packed if running is None else running, CTX, span * k, count)
               for k in range(1, radix + (running is None))]
        if running is None:
            prev_tail = got[0][state_rows, 0]
            total = sum(jnp.where(g[state_rows, 0] == prev_tail, g[:state_rows], 0.0) for g in got)
            running = jnp.concatenate([total, jnp.full((8, HEAD_DIM), prev_tail, jnp.float32)], axis=0)
            span = radix
        else:
            total = running[:state_rows] + sum(
                jnp.where(g[state_rows, 0] == prev_tail, g[:state_rows], 0.0) for g in got
            )
            running = jnp.concatenate([total, running[state_rows:]], axis=0)
            span *= radix
    return running[:state_rows].reshape(head_count, HEAD_DIM, HEAD_DIM), prev_tail


def per_device(tokens, w_qkv, out_gain, seg_ids):
    whole = lax.all_gather(tokens, "head", axis=1, tiled=True)
    w_rows = gather_weights(w_qkv)
    projected = jnp.einsum(
        "tr,grc->gtc", whole, w_rows, preferred_element_type=jnp.float32
    ).astype(jnp.bfloat16)
    row_count = seg_ids.shape[0]
    head_count = projected.shape[2] // HEAD_DIM
    queries = feature_map(projected[0]).reshape(row_count, head_count, HEAD_DIM)
    key_map = feature_map(projected[1]).reshape(row_count, head_count, HEAD_DIM)
    values = projected[2].reshape(row_count, head_count, HEAD_DIM)
    seg_float = seg_ids.astype(jnp.float32)
    tail_id = seg_float[-1]
    key_tail = jnp.where((seg_float == tail_id)[:, None, None], key_map, jnp.zeros_like(key_map))
    kv_state = jnp.einsum("thd,the->hde", key_tail, values, preferred_element_type=jnp.float32)

    state_in, tail_in = state_scan(kv_state, tail_id, row_count)

    block_rows = min(512, row_count)
    pieces = []
    for blk_no in range(row_count // block_rows):
        first_row = blk_no * block_rows
        key_end = first_row + block_rows
        query_blk = queries[first_row:key_end]
        query_pos = first_row + jnp.arange(block_rows, dtype=jnp.int32)
        query_seg = seg_float[first_row:key_end]
        scores = jnp.einsum(
            "bhd,shd->hbs", query_blk, key_map[:key_end], preferred_element_type=jnp.float32
        )
        visible = (jnp.arange(key_end, dtype=jnp.int32)[None, :] <= query_pos[:, None]) & (
            seg_float[None, :key_end] == query_seg[:, None]
        )
        weights = jnp.where(visible[None], scores, 0.0).astype(jnp.bfloat16)
        pieces.append(
            jnp.einsum("hbs,she->bhe", weights, values[:key_end], preferred_element_type=jnp.float32)
        )
    local_part = jnp.concatenate(pieces, axis=0)

    state_low = state_in.astype(jnp.bfloat16)
    prefix = jnp.einsum("thd,hde->the", queries, state_low, preferred_element_type=jnp.float32)
    prefix = jnp.where((seg_float == tail_in)[:, None, None], prefix, 0.0)
    numerator = local_part + prefix
    inv_norm = lax.rsqrt(jnp.mean(numerator * numerator, axis=-1, keepdims=True) + 1e-05)
    result = numerator * inv_norm * out_gain.reshape(head_count, HEAD_DIM)
    return result.astype(jnp.bfloat16).reshape(row_count, head_count * HEAD_DIM)


def solution(mesh):
    shape = dict(zip(mesh.axis_names, mesh.devices.shape))
    head = shape["head"]
    fine = Mesh(mesh.devices.reshape(-1, 4, 2, head), (*CTX, "head"))
    placed = (P(CTX, "head"), P(None, CTX, "head"), P("head"), P(CTX))
    return jax.shard_map(
        per_device, mesh=fine, in_specs=placed, out_specs=P(CTX, "head"), check_vma=False
    )
```

```python
import jax
import jax.numpy as jnp
from jax import lax
from jax.sharding import Mesh
from jax.sharding import PartitionSpec as P

HEAD_DIM = 128
SPAN = 16384


CTX = ("y", "x", "core")


def shifted(value, axis, steps, count):
    return lax.ppermute(value, axis, [(source, source + steps) for source in range(count - steps)])


def ring_gather(value, axis, count, dim):
    by_offset = {0: value}
    ahead = value
    behind = value
    for step in range(1, count // 2 + 1):
        ahead = lax.ppermute(ahead, axis, [(j, (j + 1) % count) for j in range(count)])
        by_offset[-step] = ahead
        if step < count - count // 2:
            behind = lax.ppermute(behind, axis, [(j, (j - 1) % count) for j in range(count)])
            by_offset[step] = behind
    low = -(count // 2)
    stacked = jnp.stack([by_offset[off] for off in range(low, low + count)], axis=0)
    ordered = jnp.roll(stacked, lax.axis_index(axis) + low, axis=0)
    moved = jnp.moveaxis(ordered, 0, dim)
    shape = list(value.shape)
    shape[dim] *= count
    return moved.reshape(shape)


def gather_weights(w_local):
    half = w_local.shape[2] // 2
    core = lax.axis_index("core")
    partner = lax.ppermute(w_local, "core", [(0, 1), (1, 0)])
    low_rows = jnp.where(core == 0, w_local[:, :, :half], partner[:, :, half:])
    high_rows = jnp.where(core == 0, partner[:, :, :half], w_local[:, :, half:])
    rows = jnp.concatenate([low_rows, high_rows], axis=1)
    rows = ring_gather(rows, "x", lax.axis_size("x"), 1)
    rows = ring_gather(rows, "y", lax.axis_size("y"), 1)
    other = lax.ppermute(rows, "core", [(0, 1), (1, 0)])
    return jnp.where(
        core == 0,
        jnp.concatenate([rows, other], axis=2),
        jnp.concatenate([other, rows], axis=2),
    )


def feature_map(values):
    return (jax.nn.elu(values.astype(jnp.float32)) + 1.0).astype(jnp.bfloat16)


def state_scan(kv_state, tail_id, row_count):
    head_count = kv_state.shape[0]
    state_rows = head_count * HEAD_DIM
    flat = kv_state.reshape(state_rows, HEAD_DIM)
    count = lax.axis_size(CTX)
    window = min(count - 1, 1 + (SPAN - 1) // row_count)
    packed = jnp.concatenate([flat, jnp.full((8, HEAD_DIM), tail_id, jnp.float32)], axis=0)
    radix = 4
    span = 1
    running = None
    while span < window:
        got = [shifted(packed if running is None else running, CTX, span * k, count)
               for k in range(1, radix + (running is None))]
        if running is None:
            prev_tail = got[0][state_rows, 0]
            total = sum(jnp.where(g[state_rows, 0] == prev_tail, g[:state_rows], 0.0) for g in got)
            running = jnp.concatenate([total, jnp.full((8, HEAD_DIM), prev_tail, jnp.float32)], axis=0)
            span = radix
        else:
            total = running[:state_rows] + sum(
                jnp.where(g[state_rows, 0] == prev_tail, g[:state_rows], 0.0) for g in got
            )
            running = jnp.concatenate([total, running[state_rows:]], axis=0)
            span *= radix
    return running[:state_rows].reshape(head_count, HEAD_DIM, HEAD_DIM), prev_tail


def per_device(tokens, w_qkv, out_gain, seg_ids):
    whole = ring_gather(tokens, "head", lax.axis_size("head"), 1)
    w_rows = gather_weights(w_qkv)
    projected = jnp.einsum(
        "tr,grc->gtc", whole, w_rows, preferred_element_type=jnp.float32
    ).astype(jnp.bfloat16)
    row_count = seg_ids.shape[0]
    head_count = projected.shape[2] // HEAD_DIM
    queries = feature_map(projected[0]).reshape(row_count, head_count, HEAD_DIM)
    key_map = feature_map(projected[1]).reshape(row_count, head_count, HEAD_DIM)
    values = projected[2].reshape(row_count, head_count, HEAD_DIM)
    seg_float = seg_ids.astype(jnp.float32)
    tail_id = seg_float[-1]
    key_tail = jnp.where((seg_float == tail_id)[:, None, None], key_map, jnp.zeros_like(key_map))
    kv_state = jnp.einsum("thd,the->hde", key_tail, values, preferred_element_type=jnp.float32)

    state_in, tail_in = state_scan(kv_state, tail_id, row_count)

    block_rows = min(512, row_count)
    pieces = []
    for blk_no in range(row_count // block_rows):
        first_row = blk_no * block_rows
        key_end = first_row + block_rows
        query_blk = queries[first_row:key_end]
        query_pos = first_row + jnp.arange(block_rows, dtype=jnp.int32)
        query_seg = seg_float[first_row:key_end]
        scores = jnp.einsum(
            "bhd,shd->hbs", query_blk, key_map[:key_end], preferred_element_type=jnp.float32
        )
        visible = (jnp.arange(key_end, dtype=jnp.int32)[None, :] <= query_pos[:, None]) & (
            seg_float[None, :key_end] == query_seg[:, None]
        )
        weights = jnp.where(visible[None], scores, 0.0).astype(jnp.bfloat16)
        pieces.append(
            jnp.einsum("hbs,she->bhe", weights, values[:key_end], preferred_element_type=jnp.float32)
        )
    local_part = jnp.concatenate(pieces, axis=0)

    state_low = state_in.astype(jnp.bfloat16)
    prefix = jnp.einsum("thd,hde->the", queries, state_low, preferred_element_type=jnp.float32)
    prefix = jnp.where((seg_float == tail_in)[:, None, None], prefix, 0.0)
    numerator = local_part + prefix
    inv_norm = lax.rsqrt(jnp.mean(numerator * numerator, axis=-1, keepdims=True) + 1e-05)
    result = numerator * inv_norm * out_gain.reshape(head_count, HEAD_DIM)
    return result.astype(jnp.bfloat16).reshape(row_count, head_count * HEAD_DIM)


def solution(mesh):
    shape = dict(zip(mesh.axis_names, mesh.devices.shape))
    head = shape["head"]
    fine = Mesh(mesh.devices.reshape(-1, 4, 2, head), (*CTX, "head"))
    placed = (P(CTX, "head"), P(None, CTX, "head"), P("head"), P(CTX))
    return jax.shard_map(
        per_device, mesh=fine, in_specs=placed, out_specs=P(CTX, "head"), check_vma=False
    )
```

```python
import jax
import jax.numpy as jnp
from jax import lax
from jax.sharding import Mesh
from jax.sharding import PartitionSpec as P

HEAD_DIM = 128
SPAN = 16384


CTX = ("y", "x", "core")


def shifted(value, axis, steps, count):
    return lax.ppermute(value, axis, [(source, source + steps) for source in range(count - steps)])


def ring_gather(value, axis, count, dim):
    by_offset = {0: value}
    ahead = value
    behind = value
    for step in range(1, count // 2 + 1):
        ahead = lax.ppermute(ahead, axis, [(j, (j + 1) % count) for j in range(count)])
        by_offset[-step] = ahead
        if step < count - count // 2:
            behind = lax.ppermute(behind, axis, [(j, (j - 1) % count) for j in range(count)])
            by_offset[step] = behind
    low = -(count // 2)
    stacked = jnp.stack([by_offset[off] for off in range(low, low + count)], axis=0)
    ordered = jnp.roll(stacked, lax.axis_index(axis) + low, axis=0)
    moved = jnp.moveaxis(ordered, 0, dim)
    shape = list(value.shape)
    shape[dim] *= count
    return moved.reshape(shape)


def gather_weights(w_local):
    half = w_local.shape[2] // 2
    core = lax.axis_index("core")
    partner = lax.ppermute(w_local, "core", [(0, 1), (1, 0)])
    low_rows = jnp.where(core == 0, w_local[:, :, :half], partner[:, :, half:])
    high_rows = jnp.where(core == 0, partner[:, :, :half], w_local[:, :, half:])
    rows = jnp.concatenate([low_rows, high_rows], axis=1)
    rows = ring_gather(rows, "x", lax.axis_size("x"), 1)
    rows = ring_gather(rows, "y", lax.axis_size("y"), 1)
    other = lax.ppermute(rows, "core", [(0, 1), (1, 0)])
    return jnp.where(
        core == 0,
        jnp.concatenate([rows, other], axis=2),
        jnp.concatenate([other, rows], axis=2),
    )


def feature_map(values):
    return (jax.nn.elu(values.astype(jnp.float32)) + 1.0).astype(jnp.bfloat16)


def state_scan(kv_state, tail_id, row_count):
    head_count = kv_state.shape[0]
    state_rows = head_count * HEAD_DIM
    flat = kv_state.reshape(state_rows, HEAD_DIM)
    count = lax.axis_size(CTX)
    window = min(count - 1, 1 + (SPAN - 1) // row_count)
    packed = jnp.concatenate([flat, jnp.full((8, HEAD_DIM), tail_id, jnp.float32)], axis=0)
    is_state = (lax.broadcasted_iota(jnp.int32, packed.shape, 0) < state_rows)
    radix = 4
    got = [shifted(packed, CTX, k, count) for k in range(1, radix + 1)]
    prev_tail = got[0][state_rows, 0]
    running = jnp.where(is_state, 0.0, prev_tail)
    for piece in got:
        running = running + jnp.where(is_state & (piece[state_rows, 0] == prev_tail), piece, 0.0)
    span = radix
    while span < window:
        got = [shifted(running, CTX, span * k, count) for k in range(1, radix)]
        for piece in got:
            running = running + jnp.where(is_state & (piece[state_rows, 0] == prev_tail), piece, 0.0)
        span *= radix
    return running[:state_rows].reshape(head_count, HEAD_DIM, HEAD_DIM), prev_tail


def per_device(tokens, w_qkv, out_gain, seg_ids):
    whole = lax.all_gather(tokens, "head", axis=1, tiled=True)
    w_rows = gather_weights(w_qkv)
    key_value = jnp.einsum(
        "tr,grc->gtc", whole, w_rows[1:], preferred_element_type=jnp.float32
    ).astype(jnp.bfloat16)
    row_count = seg_ids.shape[0]
    head_count = key_value.shape[2] // HEAD_DIM
    key_map = feature_map(key_value[0]).reshape(row_count, head_count, HEAD_DIM)
    values = key_value[1].reshape(row_count, head_count, HEAD_DIM)
    seg_float = seg_ids.astype(jnp.float32)
    tail_id = seg_float[-1]
    key_tail = jnp.where((seg_float == tail_id)[:, None, None], key_map, jnp.zeros_like(key_map))
    kv_state = jnp.einsum("thd,the->hde", key_tail, values, preferred_element_type=jnp.float32)

    state_in, tail_in = state_scan(kv_state, tail_id, row_count)
    query_proj = jnp.einsum("tr,rc->tc", whole, w_rows[0], preferred_element_type=jnp.float32)
    queries = feature_map(query_proj.astype(jnp.bfloat16)).reshape(row_count, head_count, HEAD_DIM)

    block_rows = min(512, row_count)
    pieces = []
    for blk_no in range(row_count // block_rows):
        first_row = blk_no * block_rows
        key_end = first_row + block_rows
        query_blk = queries[first_row:key_end]
        query_pos = first_row + jnp.arange(block_rows, dtype=jnp.int32)
        query_seg = seg_float[first_row:key_end]
        scores = jnp.einsum(
            "bhd,shd->hbs", query_blk, key_map[:key_end], preferred_element_type=jnp.float32
        )
        visible = (jnp.arange(key_end, dtype=jnp.int32)[None, :] <= query_pos[:, None]) & (
            seg_float[None, :key_end] == query_seg[:, None]
        )
        weights = jnp.where(visible[None], scores, 0.0).astype(jnp.bfloat16)
        pieces.append(
            jnp.einsum("hbs,she->bhe", weights, values[:key_end], preferred_element_type=jnp.float32)
        )
    local_part = jnp.concatenate(pieces, axis=0)

    state_low = state_in.astype(jnp.bfloat16)
    prefix = jnp.einsum("thd,hde->the", queries, state_low, preferred_element_type=jnp.float32)
    prefix = jnp.where((seg_float == tail_in)[:, None, None], prefix, 0.0)
    numerator = local_part + prefix
    inv_norm = lax.rsqrt(jnp.mean(numerator * numerator, axis=-1, keepdims=True) + 1e-05)
    result = numerator * inv_norm * out_gain.reshape(head_count, HEAD_DIM)
    return result.astype(jnp.bfloat16).reshape(row_count, head_count * HEAD_DIM)


def solution(mesh):
    shape = dict(zip(mesh.axis_names, mesh.devices.shape))
    head = shape["head"]
    fine = Mesh(mesh.devices.reshape(-1, 4, 2, head), (*CTX, "head"))
    placed = (P(CTX, "head"), P(None, CTX, "head"), P("head"), P(CTX))
    return jax.shard_map(
        per_device, mesh=fine, in_specs=placed, out_specs=P(CTX, "head"), check_vma=False
    )
```

```python
import jax
import jax.numpy as jnp
from jax import lax
from jax.sharding import Mesh
from jax.sharding import PartitionSpec as P

HEAD_DIM = 128
SPAN = 16384


CTX = ("y", "x", "core")


def shifted(value, axis, steps, count):
    return lax.ppermute(value, axis, [(source, source + steps) for source in range(count - steps)])


def ring_gather(value, axis, count, dim):
    by_offset = {0: value}
    ahead = value
    behind = value
    for step in range(1, count // 2 + 1):
        ahead = lax.ppermute(ahead, axis, [(j, (j + 1) % count) for j in range(count)])
        by_offset[-step] = ahead
        if step < count - count // 2:
            behind = lax.ppermute(behind, axis, [(j, (j - 1) % count) for j in range(count)])
            by_offset[step] = behind
    low = -(count // 2)
    stacked = jnp.stack([by_offset[off] for off in range(low, low + count)], axis=0)
    ordered = jnp.roll(stacked, lax.axis_index(axis) + low, axis=0)
    moved = jnp.moveaxis(ordered, 0, dim)
    shape = list(value.shape)
    shape[dim] *= count
    return moved.reshape(shape)


def gather_weights(w_local):
    half = w_local.shape[2] // 2
    core = lax.axis_index("core")
    partner = lax.ppermute(w_local, "core", [(0, 1), (1, 0)])
    low_rows = jnp.where(core == 0, w_local[:, :, :half], partner[:, :, half:])
    high_rows = jnp.where(core == 0, partner[:, :, :half], w_local[:, :, half:])
    rows = jnp.concatenate([low_rows, high_rows], axis=1)
    rows = ring_gather(rows, "x", lax.axis_size("x"), 1)
    rows = ring_gather(rows, "y", lax.axis_size("y"), 1)
    other = lax.ppermute(rows, "core", [(0, 1), (1, 0)])
    return jnp.where(
        core == 0,
        jnp.concatenate([rows, other], axis=2),
        jnp.concatenate([other, rows], axis=2),
    )


def feature_map(values):
    return (jax.nn.elu(values.astype(jnp.float32)) + 1.0).astype(jnp.bfloat16)


def state_scan(kv_state, tails, row_count):
    count = lax.axis_size(CTX)
    window = min(count - 1, 1 + (SPAN - 1) // row_count)
    me = lax.axis_index(CTX)

    def tail_of(block):
        return jnp.where(block >= 0, tails[jnp.clip(block, 0, count - 1)], -1.0)

    prev_tail = tail_of(me - 1)

    def counts(block):
        return (block >= 0) & (tail_of(block) == prev_tail)

    radix = 4
    got = [shifted(kv_state, CTX, k, count) for k in range(1, radix + 1)]
    running = sum(jnp.where(counts(me - k), piece, 0.0) for k, piece in zip(range(1, radix + 1), got))
    span = radix
    while span < window:
        got = [shifted(running, CTX, span * k, count) for k in range(1, radix)]
        running = running + sum(
            jnp.where(counts(me - span * k - 1), piece, 0.0) for k, piece in zip(range(1, radix), got)
        )
        span *= radix
    return running, prev_tail


def per_device(tokens, w_qkv, out_gain, seg_ids):
    whole = lax.all_gather(tokens, "head", axis=1, tiled=True)
    row_count = seg_ids.shape[0]
    groups = lax.axis_size(CTX)
    own_rows = w_qkv.shape[1]
    tail_row = jnp.full((w_qkv.shape[0], 1, w_qkv.shape[2]), seg_ids[-1], w_qkv.dtype)
    carried = gather_weights(jnp.concatenate([w_qkv, tail_row], axis=1))
    carried = carried.reshape(w_qkv.shape[0], groups, own_rows + 1, w_qkv.shape[2])
    w_rows = carried[:, :, :own_rows].reshape(w_qkv.shape[0], groups * own_rows, w_qkv.shape[2])
    tails = carried[0, :, own_rows, 0].astype(jnp.float32)
    key_value = jnp.einsum(
        "tr,grc->gtc", whole, w_rows[1:], preferred_element_type=jnp.float32
    ).astype(jnp.bfloat16)
    head_count = key_value.shape[2] // HEAD_DIM
    key_map = feature_map(key_value[0]).reshape(row_count, head_count, HEAD_DIM)
    values = key_value[1].reshape(row_count, head_count, HEAD_DIM)
    seg_float = seg_ids.astype(jnp.float32)
    tail_id = seg_float[-1]
    key_tail = jnp.where((seg_float == tail_id)[:, None, None], key_map, jnp.zeros_like(key_map))
    kv_state = jnp.einsum("thd,the->hde", key_tail, values, preferred_element_type=jnp.float32)

    state_in, tail_in = state_scan(kv_state, tails, row_count)
    query_proj = jnp.einsum("tr,rc->tc", whole, w_rows[0], preferred_element_type=jnp.float32)
    query_proj = lax.reduce_precision(query_proj, exponent_bits=8, mantissa_bits=7)
    queries = feature_map(query_proj).reshape(row_count, head_count, HEAD_DIM)

    block_rows = min(512, row_count)
    pieces = []
    for blk_no in range(row_count // block_rows):
        first_row = blk_no * block_rows
        key_end = first_row + block_rows
        query_blk = queries[first_row:key_end]
        query_pos = first_row + jnp.arange(block_rows, dtype=jnp.int32)
        query_seg = seg_float[first_row:key_end]
        scores = jnp.einsum(
            "bhd,shd->hbs", query_blk, key_map[:key_end], preferred_element_type=jnp.float32
        )
        visible = (jnp.arange(key_end, dtype=jnp.int32)[None, :] <= query_pos[:, None]) & (
            seg_float[None, :key_end] == query_seg[:, None]
        )
        weights = jnp.where(visible[None], scores, 0.0).astype(jnp.bfloat16)
        pieces.append(
            jnp.einsum("hbs,she->bhe", weights, values[:key_end], preferred_element_type=jnp.float32)
        )
    local_part = jnp.concatenate(pieces, axis=0)

    state_low = state_in.astype(jnp.bfloat16)
    prefix = jnp.einsum("thd,hde->the", queries, state_low, preferred_element_type=jnp.float32)
    prefix = jnp.where((seg_float == tail_in)[:, None, None], prefix, 0.0)
    numerator = local_part + prefix
    inv_norm = lax.rsqrt(jnp.mean(numerator * numerator, axis=-1, keepdims=True) + 1e-05)
    result = numerator * inv_norm * out_gain.reshape(head_count, HEAD_DIM)
    return result.astype(jnp.bfloat16).reshape(row_count, head_count * HEAD_DIM)


def solution(mesh):
    shape = dict(zip(mesh.axis_names, mesh.devices.shape))
    head = shape["head"]
    fine = Mesh(mesh.devices.reshape(-1, 4, 2, head), (*CTX, "head"))
    placed = (P(CTX, "head"), P(None, CTX, "head"), P("head"), P(CTX))
    return jax.shard_map(
        per_device, mesh=fine, in_specs=placed, out_specs=P(CTX, "head"), check_vma=False
    )
```

```python
import jax
import jax.numpy as jnp
from jax import lax
from jax.sharding import Mesh
from jax.sharding import PartitionSpec as P

HEAD_DIM = 128
SPAN = 16384


CTX = ("y", "x", "core")


def shifted(value, axis, steps, count):
    return lax.ppermute(value, axis, [(source, source + steps) for source in range(count - steps)])


def ring_gather(value, axis, count, dim):
    by_offset = {0: value}
    ahead = value
    behind = value
    for step in range(1, count // 2 + 1):
        ahead = lax.ppermute(ahead, axis, [(j, (j + 1) % count) for j in range(count)])
        by_offset[-step] = ahead
        if step < count - count // 2:
            behind = lax.ppermute(behind, axis, [(j, (j - 1) % count) for j in range(count)])
            by_offset[step] = behind
    low = -(count // 2)
    stacked = jnp.stack([by_offset[off] for off in range(low, low + count)], axis=0)
    ordered = jnp.roll(stacked, lax.axis_index(axis) + low, axis=0)
    moved = jnp.moveaxis(ordered, 0, dim)
    shape = list(value.shape)
    shape[dim] *= count
    return moved.reshape(shape)


def gather_weights(w_local):
    half = w_local.shape[2] // 2
    core = lax.axis_index("core")
    partner = lax.ppermute(w_local, "core", [(0, 1), (1, 0)])
    low_rows = jnp.where(core == 0, w_local[:, :, :half], partner[:, :, half:])
    high_rows = jnp.where(core == 0, partner[:, :, :half], w_local[:, :, half:])
    rows = jnp.concatenate([low_rows, high_rows], axis=1)
    rows = ring_gather(rows, "x", lax.axis_size("x"), 1)
    rows = ring_gather(rows, "y", lax.axis_size("y"), 1)
    other = lax.ppermute(rows, "core", [(0, 1), (1, 0)])
    return jnp.where(
        core == 0,
        jnp.concatenate([rows, other], axis=2),
        jnp.concatenate([other, rows], axis=2),
    )


def feature_map(values):
    return (jax.nn.elu(values.astype(jnp.float32)) + 1.0).astype(jnp.bfloat16)


def state_scan(kv_state, tails, row_count):
    count = lax.axis_size(CTX)
    window = min(count - 1, 1 + (SPAN - 1) // row_count)
    me = lax.axis_index(CTX)

    def tail_of(block):
        return jnp.where(block >= 0, tails[jnp.clip(block, 0, count - 1)], -1.0)

    prev_tail = tail_of(me - 1)

    def counts(block):
        return (block >= 0) & (tail_of(block) == prev_tail)

    radix = 4
    got = [shifted(kv_state, CTX, k, count) for k in range(1, radix + 1)]
    running = sum(jnp.where(counts(me - k), piece, 0.0) for k, piece in zip(range(1, radix + 1), got))
    span = radix
    while span < window:
        got = [shifted(running, CTX, span * k, count) for k in range(1, radix)]
        running = running + sum(
            jnp.where(counts(me - span * k - 1), piece, 0.0) for k, piece in zip(range(1, radix), got)
        )
        span *= radix
    return running, prev_tail


def per_device(tokens, w_qkv, out_gain, seg_ids):
    half_rows = tokens.shape[0] // 2
    whole = jnp.concatenate([
        lax.all_gather(tokens[:half_rows], "head", axis=1, tiled=True),
        lax.all_gather(tokens[half_rows:], "head", axis=1, tiled=True)], axis=0)
    row_count = seg_ids.shape[0]
    groups = lax.axis_size(CTX)
    own_rows = w_qkv.shape[1]
    tail_row = jnp.full((w_qkv.shape[0], 1, w_qkv.shape[2]), seg_ids[-1], w_qkv.dtype)
    carried = gather_weights(jnp.concatenate([w_qkv, tail_row], axis=1))
    carried = carried.reshape(w_qkv.shape[0], groups, own_rows + 1, w_qkv.shape[2])
    w_rows = carried[:, :, :own_rows].reshape(w_qkv.shape[0], groups * own_rows, w_qkv.shape[2])
    tails = carried[0, :, own_rows, 0].astype(jnp.float32)
    key_value = jnp.einsum(
        "tr,grc->gtc", whole, w_rows[1:], preferred_element_type=jnp.float32
    ).astype(jnp.bfloat16)
    head_count = key_value.shape[2] // HEAD_DIM
    key_map = feature_map(key_value[0]).reshape(row_count, head_count, HEAD_DIM)
    values = key_value[1].reshape(row_count, head_count, HEAD_DIM)
    seg_float = seg_ids.astype(jnp.float32)
    tail_id = seg_float[-1]
    key_tail = jnp.where((seg_float == tail_id)[:, None, None], key_map, jnp.zeros_like(key_map))
    kv_state = jnp.einsum("thd,the->hde", key_tail, values, preferred_element_type=jnp.float32)

    state_in, tail_in = state_scan(kv_state, tails, row_count)
    query_proj = jnp.einsum("tr,rc->tc", whole, w_rows[0], preferred_element_type=jnp.float32)
    query_proj = lax.reduce_precision(query_proj, exponent_bits=8, mantissa_bits=7)
    queries = feature_map(query_proj).reshape(row_count, head_count, HEAD_DIM)

    block_rows = min(512, row_count)
    pieces = []
    for blk_no in range(row_count // block_rows):
        first_row = blk_no * block_rows
        key_end = first_row + block_rows
        query_blk = queries[first_row:key_end]
        query_pos = first_row + jnp.arange(block_rows, dtype=jnp.int32)
        query_seg = seg_float[first_row:key_end]
        scores = jnp.einsum(
            "bhd,shd->hbs", query_blk, key_map[:key_end], preferred_element_type=jnp.float32
        )
        visible = (jnp.arange(key_end, dtype=jnp.int32)[None, :] <= query_pos[:, None]) & (
            seg_float[None, :key_end] == query_seg[:, None]
        )
        weights = jnp.where(visible[None], scores, 0.0).astype(jnp.bfloat16)
        pieces.append(
            jnp.einsum("hbs,she->bhe", weights, values[:key_end], preferred_element_type=jnp.float32)
        )
    local_part = jnp.concatenate(pieces, axis=0)

    state_low = state_in.astype(jnp.bfloat16)
    prefix = jnp.einsum("thd,hde->the", queries, state_low, preferred_element_type=jnp.float32)
    prefix = jnp.where((seg_float == tail_in)[:, None, None], prefix, 0.0)
    numerator = local_part + prefix
    inv_norm = lax.rsqrt(jnp.mean(numerator * numerator, axis=-1, keepdims=True) + 1e-05)
    result = numerator * inv_norm * out_gain.reshape(head_count, HEAD_DIM)
    return result.astype(jnp.bfloat16).reshape(row_count, head_count * HEAD_DIM)


def solution(mesh):
    shape = dict(zip(mesh.axis_names, mesh.devices.shape))
    head = shape["head"]
    fine = Mesh(mesh.devices.reshape(-1, 4, 2, head), (*CTX, "head"))
    placed = (P(CTX, "head"), P(None, CTX, "head"), P("head"), P(CTX))
    return jax.shard_map(
        per_device, mesh=fine, in_specs=placed, out_specs=P(CTX, "head"), check_vma=False
    )
```

```python
import jax
import jax.numpy as jnp
from jax import lax
from jax.sharding import Mesh
from jax.sharding import PartitionSpec as P

HEAD_DIM = 128
SPAN = 16384


CTX = ("y", "x", "core")


def shifted(value, axis, steps, count):
    return lax.ppermute(value, axis, [(source, source + steps) for source in range(count - steps)])


def ring_gather(value, axis, count, dim):
    by_offset = {0: value}
    ahead = value
    behind = value
    for step in range(1, count // 2 + 1):
        ahead = lax.ppermute(ahead, axis, [(j, (j + 1) % count) for j in range(count)])
        by_offset[-step] = ahead
        if step < count - count // 2:
            behind = lax.ppermute(behind, axis, [(j, (j - 1) % count) for j in range(count)])
            by_offset[step] = behind
    low = -(count // 2)
    stacked = jnp.stack([by_offset[off] for off in range(low, low + count)], axis=0)
    ordered = jnp.roll(stacked, lax.axis_index(axis) + low, axis=0)
    moved = jnp.moveaxis(ordered, 0, dim)
    shape = list(value.shape)
    shape[dim] *= count
    return moved.reshape(shape)


def gather_weights(w_local):
    half = w_local.shape[2] // 2
    core = lax.axis_index("core")
    partner = lax.ppermute(w_local, "core", [(0, 1), (1, 0)])
    low_rows = jnp.where(core == 0, w_local[:, :, :half], partner[:, :, half:])
    high_rows = jnp.where(core == 0, partner[:, :, :half], w_local[:, :, half:])
    rows = jnp.concatenate([low_rows, high_rows], axis=1)
    rows = ring_gather(rows, "x", lax.axis_size("x"), 1)
    rows = ring_gather(rows, "y", lax.axis_size("y"), 1)
    other = lax.ppermute(rows, "core", [(0, 1), (1, 0)])
    return jnp.where(
        core == 0,
        jnp.concatenate([rows, other], axis=2),
        jnp.concatenate([other, rows], axis=2),
    )


def feature_map(values):
    return (jax.nn.elu(values.astype(jnp.float32)) + 1.0).astype(jnp.bfloat16)


def state_scan(kv_state, tails, row_count):
    count = lax.axis_size(CTX)
    window = min(count - 1, 1 + (SPAN - 1) // row_count)
    row_len = lax.axis_size("x") * lax.axis_size("core")
    assert window <= 2 * row_len
    me = lax.axis_index(CTX)
    pos = me % row_len
    first = me - pos

    def tail_of(block):
        return jnp.where(block >= 0, tails[jnp.clip(block, 0, count - 1)], -1.0)

    prev_tail = tail_of(me - 1)
    spread = jnp.broadcast_to(kv_state[None], (row_len,) + kv_state.shape)
    row = lax.all_to_all(spread, ("x", "core"), 0, 0, tiled=True)
    places = jnp.arange(row_len)
    row_tails = tail_of(first + places)
    in_last = row_tails == row_tails[row_len - 1]

    def masked(mask):
        return jnp.sum(jnp.where(mask[:, None, None, None], row, 0.0), axis=0)

    y_count = lax.axis_size("y")
    one_back = shifted(masked(in_last), "y", 1, y_count)
    two_back = shifted(masked(in_last & (places >= pos)), "y", 2, y_count)
    state = masked((places < pos) & (row_tails == prev_tail))
    state = state + jnp.where(tail_of(first - 1) == prev_tail, one_back, 0.0)
    if window > row_len:
        state = state + jnp.where(tail_of(first - row_len - 1) == prev_tail, two_back, 0.0)
    return state, prev_tail


def per_device(tokens, w_qkv, out_gain, seg_ids):
    whole = lax.all_gather(tokens, "head", axis=1, tiled=True)
    row_count = seg_ids.shape[0]
    groups = lax.axis_size(CTX)
    own_rows = w_qkv.shape[1]
    tail_row = jnp.full((w_qkv.shape[0], 1, w_qkv.shape[2]), seg_ids[-1], w_qkv.dtype)
    carried = gather_weights(jnp.concatenate([w_qkv, tail_row], axis=1))
    carried = carried.reshape(w_qkv.shape[0], groups, own_rows + 1, w_qkv.shape[2])
    w_rows = carried[:, :, :own_rows].reshape(w_qkv.shape[0], groups * own_rows, w_qkv.shape[2])
    tails = carried[0, :, own_rows, 0].astype(jnp.float32)
    key_value = jnp.einsum(
        "tr,grc->gtc", whole, w_rows[1:], preferred_element_type=jnp.float32
    ).astype(jnp.bfloat16)
    head_count = key_value.shape[2] // HEAD_DIM
    key_map = feature_map(key_value[0]).reshape(row_count, head_count, HEAD_DIM)
    values = key_value[1].reshape(row_count, head_count, HEAD_DIM)
    seg_float = seg_ids.astype(jnp.float32)
    tail_id = seg_float[-1]
    key_tail = jnp.where((seg_float == tail_id)[:, None, None], key_map, jnp.zeros_like(key_map))
    kv_state = jnp.einsum("thd,the->hde", key_tail, values, preferred_element_type=jnp.float32)

    state_in, tail_in = state_scan(kv_state, tails, row_count)
    query_proj = jnp.einsum("tr,rc->tc", whole, w_rows[0], preferred_element_type=jnp.float32)
    query_proj = lax.reduce_precision(query_proj, exponent_bits=8, mantissa_bits=7)
    queries = feature_map(query_proj).reshape(row_count, head_count, HEAD_DIM)

    block_rows = min(512, row_count)
    pieces = []
    for blk_no in range(row_count // block_rows):
        first_row = blk_no * block_rows
        key_end = first_row + block_rows
        query_blk = queries[first_row:key_end]
        query_pos = first_row + jnp.arange(block_rows, dtype=jnp.int32)
        query_seg = seg_float[first_row:key_end]
        scores = jnp.einsum(
            "bhd,shd->hbs", query_blk, key_map[:key_end], preferred_element_type=jnp.float32
        )
        visible = (jnp.arange(key_end, dtype=jnp.int32)[None, :] <= query_pos[:, None]) & (
            seg_float[None, :key_end] == query_seg[:, None]
        )
        weights = jnp.where(visible[None], scores, 0.0).astype(jnp.bfloat16)
        pieces.append(
            jnp.einsum("hbs,she->bhe", weights, values[:key_end], preferred_element_type=jnp.float32)
        )
    local_part = jnp.concatenate(pieces, axis=0)

    state_low = state_in.astype(jnp.bfloat16)
    prefix = jnp.einsum("thd,hde->the", queries, state_low, preferred_element_type=jnp.float32)
    prefix = jnp.where((seg_float == tail_in)[:, None, None], prefix, 0.0)
    numerator = local_part + prefix
    inv_norm = lax.rsqrt(jnp.mean(numerator * numerator, axis=-1, keepdims=True) + 1e-05)
    result = numerator * inv_norm * out_gain.reshape(head_count, HEAD_DIM)
    return result.astype(jnp.bfloat16).reshape(row_count, head_count * HEAD_DIM)


def solution(mesh):
    shape = dict(zip(mesh.axis_names, mesh.devices.shape))
    head = shape["head"]
    fine = Mesh(mesh.devices.reshape(-1, 4, 2, head), (*CTX, "head"))
    placed = (P(CTX, "head"), P(None, CTX, "head"), P("head"), P(CTX))
    return jax.shard_map(
        per_device, mesh=fine, in_specs=placed, out_specs=P(CTX, "head"), check_vma=False
    )
```

```python
import jax
import jax.numpy as jnp
from jax import lax
from jax.sharding import Mesh
from jax.sharding import PartitionSpec as P

HEAD_DIM = 128
SPAN = 16384


CTX = ("y", "x", "core")


def shifted(value, axis, steps, count):
    return lax.ppermute(value, axis, [(source, source + steps) for source in range(count - steps)])


def ring_gather(value, axis, count, dim):
    by_offset = {0: value}
    ahead = value
    behind = value
    for step in range(1, count // 2 + 1):
        ahead = lax.ppermute(ahead, axis, [(j, (j + 1) % count) for j in range(count)])
        by_offset[-step] = ahead
        if step < count - count // 2:
            behind = lax.ppermute(behind, axis, [(j, (j - 1) % count) for j in range(count)])
            by_offset[step] = behind
    low = -(count // 2)
    stacked = jnp.stack([by_offset[off] for off in range(low, low + count)], axis=0)
    ordered = jnp.roll(stacked, lax.axis_index(axis) + low, axis=0)
    moved = jnp.moveaxis(ordered, 0, dim)
    shape = list(value.shape)
    shape[dim] *= count
    return moved.reshape(shape)


def gather_weights(w_local):
    half = w_local.shape[2] // 2
    core = lax.axis_index("core")
    partner = lax.ppermute(w_local, "core", [(0, 1), (1, 0)])
    low_rows = jnp.where(core == 0, w_local[:, :, :half], partner[:, :, half:])
    high_rows = jnp.where(core == 0, partner[:, :, :half], w_local[:, :, half:])
    rows = jnp.concatenate([low_rows, high_rows], axis=1)
    rows = ring_gather(rows, "x", lax.axis_size("x"), 1)
    rows = ring_gather(rows, "y", lax.axis_size("y"), 1)
    other = lax.ppermute(rows, "core", [(0, 1), (1, 0)])
    return jnp.where(
        core == 0,
        jnp.concatenate([rows, other], axis=2),
        jnp.concatenate([other, rows], axis=2),
    )


def feature_map(values):
    return (jax.nn.elu(values.astype(jnp.float32)) + 1.0).astype(jnp.bfloat16)


def state_scan(kv_state, tails, row_count):
    count = lax.axis_size(CTX)
    window = min(count - 1, 1 + (SPAN - 1) // row_count)
    row_len = lax.axis_size("x") * lax.axis_size("core")
    assert window <= 2 * row_len
    me = lax.axis_index(CTX)
    pos = me % row_len
    first = me - pos

    def tail_of(block):
        return jnp.where(block >= 0, tails[jnp.clip(block, 0, count - 1)], -1.0)

    prev_tail = tail_of(me - 1)
    spread = jnp.broadcast_to(kv_state[None], (row_len,) + kv_state.shape)
    row = lax.all_to_all(spread, ("x", "core"), 0, 0, tiled=True)
    places = jnp.arange(row_len)
    row_tails = tail_of(first + places)
    in_last = row_tails == row_tails[row_len - 1]

    def masked(mask):
        return jnp.sum(jnp.where(mask[:, None, None, None], row, 0.0), axis=0)

    y_count = lax.axis_size("y")
    one_back = shifted(masked(in_last), "y", 1, y_count)
    two_back = shifted(masked(in_last & (places >= pos)), "y", 2, y_count)
    state = masked((places < pos) & (row_tails == prev_tail))
    state = state + jnp.where(tail_of(first - 1) == prev_tail, one_back, 0.0)
    if window > row_len:
        state = state + jnp.where(tail_of(first - row_len - 1) == prev_tail, two_back, 0.0)
    return state, prev_tail


def per_device(tokens, w_qkv, out_gain, seg_ids):
    whole = lax.all_gather(tokens, "head", axis=1, tiled=True)
    row_count = seg_ids.shape[0]
    groups = lax.axis_size(CTX)
    own_rows = w_qkv.shape[1]
    tail_row = jnp.full((w_qkv.shape[0], 1, w_qkv.shape[2]), seg_ids[-1], w_qkv.dtype)
    carried = gather_weights(jnp.concatenate([w_qkv, tail_row], axis=1))
    carried = carried.reshape(w_qkv.shape[0], groups, own_rows + 1, w_qkv.shape[2])
    w_rows = carried[:, :, :own_rows].reshape(w_qkv.shape[0], groups * own_rows, w_qkv.shape[2])
    tails = carried[0, :, own_rows, 0].astype(jnp.float32)
    key_value = jnp.einsum(
        "tr,grc->gtc", whole, w_rows[1:], preferred_element_type=jnp.float32
    ).astype(jnp.bfloat16)
    head_count = key_value.shape[2] // HEAD_DIM
    key_map = feature_map(key_value[0]).reshape(row_count, head_count, HEAD_DIM)
    values = key_value[1].reshape(row_count, head_count, HEAD_DIM)
    seg_float = seg_ids.astype(jnp.float32)
    tail_id = seg_float[-1]
    key_tail = jnp.where((seg_float == tail_id)[:, None, None], key_map, jnp.zeros_like(key_map))
    kv_state = jnp.einsum("thd,the->hde", key_tail, values, preferred_element_type=jnp.float32)

    tails, kv_state = lax.optimization_barrier((tails, kv_state))
    state_in, tail_in = state_scan(kv_state, tails, row_count)
    query_proj = jnp.einsum("tr,rc->tc", whole, w_rows[0], preferred_element_type=jnp.float32)
    query_proj = lax.reduce_precision(query_proj, exponent_bits=8, mantissa_bits=7)
    queries = feature_map(query_proj).reshape(row_count, head_count, HEAD_DIM)

    block_rows = min(512, row_count)
    pieces = []
    for blk_no in range(row_count // block_rows):
        first_row = blk_no * block_rows
        key_end = first_row + block_rows
        query_blk = queries[first_row:key_end]
        query_pos = first_row + jnp.arange(block_rows, dtype=jnp.int32)
        query_seg = seg_float[first_row:key_end]
        scores = jnp.einsum(
            "bhd,shd->hbs", query_blk, key_map[:key_end], preferred_element_type=jnp.float32
        )
        visible = (jnp.arange(key_end, dtype=jnp.int32)[None, :] <= query_pos[:, None]) & (
            seg_float[None, :key_end] == query_seg[:, None]
        )
        weights = jnp.where(visible[None], scores, 0.0).astype(jnp.bfloat16)
        pieces.append(
            jnp.einsum("hbs,she->bhe", weights, values[:key_end], preferred_element_type=jnp.float32)
        )
    local_part = jnp.concatenate(pieces, axis=0)

    state_low = state_in.astype(jnp.bfloat16)
    prefix = jnp.einsum("thd,hde->the", queries, state_low, preferred_element_type=jnp.float32)
    prefix = jnp.where((seg_float == tail_in)[:, None, None], prefix, 0.0)
    numerator = local_part + prefix
    inv_norm = lax.rsqrt(jnp.mean(numerator * numerator, axis=-1, keepdims=True) + 1e-05)
    result = numerator * inv_norm * out_gain.reshape(head_count, HEAD_DIM)
    return result.astype(jnp.bfloat16).reshape(row_count, head_count * HEAD_DIM)


def solution(mesh):
    shape = dict(zip(mesh.axis_names, mesh.devices.shape))
    head = shape["head"]
    fine = Mesh(mesh.devices.reshape(-1, 4, 2, head), (*CTX, "head"))
    placed = (P(CTX, "head"), P(None, CTX, "head"), P("head"), P(CTX))
    return jax.shard_map(
        per_device, mesh=fine, in_specs=placed, out_specs=P(CTX, "head"), check_vma=False
    )
```

```python
import jax
import jax.numpy as jnp
from jax import lax
from jax.sharding import Mesh
from jax.sharding import PartitionSpec as P

HEAD_DIM = 128
SPAN = 16384


CTX = ("y", "x", "core")


def shifted(value, axis, steps, count):
    return lax.ppermute(value, axis, [(source, source + steps) for source in range(count - steps)])


def ring_gather(value, axis, count, dim):
    by_offset = {0: value}
    ahead = value
    behind = value
    for step in range(1, count // 2 + 1):
        ahead = lax.ppermute(ahead, axis, [(j, (j + 1) % count) for j in range(count)])
        by_offset[-step] = ahead
        if step < count - count // 2:
            behind = lax.ppermute(behind, axis, [(j, (j - 1) % count) for j in range(count)])
            by_offset[step] = behind
    low = -(count // 2)
    stacked = jnp.stack([by_offset[off] for off in range(low, low + count)], axis=0)
    ordered = jnp.roll(stacked, lax.axis_index(axis) + low, axis=0)
    moved = jnp.moveaxis(ordered, 0, dim)
    shape = list(value.shape)
    shape[dim] *= count
    return moved.reshape(shape)


def gather_weights(w_local):
    half = w_local.shape[2] // 2
    core = lax.axis_index("core")
    partner = lax.ppermute(w_local, "core", [(0, 1), (1, 0)])
    low_rows = jnp.where(core == 0, w_local[:, :, :half], partner[:, :, half:])
    high_rows = jnp.where(core == 0, partner[:, :, :half], w_local[:, :, half:])
    rows = jnp.concatenate([low_rows, high_rows], axis=1)
    rows = ring_gather(rows, "x", lax.axis_size("x"), 1)
    rows = ring_gather(rows, "y", lax.axis_size("y"), 1)
    other = lax.ppermute(rows, "core", [(0, 1), (1, 0)])
    return jnp.where(
        core == 0,
        jnp.concatenate([rows, other], axis=2),
        jnp.concatenate([other, rows], axis=2),
    )


def feature_map(values):
    return (jax.nn.elu(values.astype(jnp.float32)) + 1.0).astype(jnp.bfloat16)


def state_scan(kv_state, tails, row_count):
    count = lax.axis_size(CTX)
    window = min(count - 1, 1 + (SPAN - 1) // row_count)
    row_len = lax.axis_size("x") * lax.axis_size("core")
    assert window <= 2 * row_len
    me = lax.axis_index(CTX)
    pos = me % row_len
    first = me - pos

    def tail_of(block):
        return jnp.where(block >= 0, tails[jnp.clip(block, 0, count - 1)], -1.0)

    prev_tail = tail_of(me - 1)
    spread = jnp.broadcast_to(kv_state.astype(jnp.bfloat16)[None], (row_len,) + kv_state.shape)
    row = lax.all_to_all(spread, ("x", "core"), 0, 0, tiled=True).astype(jnp.float32)
    places = jnp.arange(row_len)
    row_tails = tail_of(first + places)
    in_last = row_tails == row_tails[row_len - 1]

    def masked(mask):
        return jnp.sum(jnp.where(mask[:, None, None, None], row, 0.0), axis=0)

    y_count = lax.axis_size("y")
    one_back = shifted(masked(in_last).astype(jnp.bfloat16), "y", 1, y_count).astype(jnp.float32)
    two_back = shifted(
        masked(in_last & (places >= pos)).astype(jnp.bfloat16), "y", 2, y_count
    ).astype(jnp.float32)
    state = masked((places < pos) & (row_tails == prev_tail))
    state = state + jnp.where(tail_of(first - 1) == prev_tail, one_back, 0.0)
    if window > row_len:
        state = state + jnp.where(tail_of(first - row_len - 1) == prev_tail, two_back, 0.0)
    return state, prev_tail


def per_device(tokens, w_qkv, out_gain, seg_ids):
    whole = lax.all_gather(tokens, "head", axis=1, tiled=True)
    row_count = seg_ids.shape[0]
    groups = lax.axis_size(CTX)
    own_rows = w_qkv.shape[1]
    tail_row = jnp.full((w_qkv.shape[0], 1, w_qkv.shape[2]), seg_ids[-1], w_qkv.dtype)
    carried = gather_weights(jnp.concatenate([w_qkv, tail_row], axis=1))
    carried = carried.reshape(w_qkv.shape[0], groups, own_rows + 1, w_qkv.shape[2])
    w_rows = carried[:, :, :own_rows].reshape(w_qkv.shape[0], groups * own_rows, w_qkv.shape[2])
    tails = carried[0, :, own_rows, 0].astype(jnp.float32)
    key_value = jnp.einsum(
        "tr,grc->gtc", whole, w_rows[1:], preferred_element_type=jnp.float32
    ).astype(jnp.bfloat16)
    head_count = key_value.shape[2] // HEAD_DIM
    key_map = feature_map(key_value[0]).reshape(row_count, head_count, HEAD_DIM)
    values = key_value[1].reshape(row_count, head_count, HEAD_DIM)
    seg_float = seg_ids.astype(jnp.float32)
    tail_id = seg_float[-1]
    key_tail = jnp.where((seg_float == tail_id)[:, None, None], key_map, jnp.zeros_like(key_map))
    kv_state = jnp.einsum("thd,the->hde", key_tail, values, preferred_element_type=jnp.float32)

    tails, kv_state = lax.optimization_barrier((tails, kv_state))
    state_in, tail_in = state_scan(kv_state, tails, row_count)
    query_proj = jnp.einsum("tr,rc->tc", whole, w_rows[0], preferred_element_type=jnp.float32)
    query_proj = lax.reduce_precision(query_proj, exponent_bits=8, mantissa_bits=7)
    queries = feature_map(query_proj).reshape(row_count, head_count, HEAD_DIM)

    block_rows = min(512, row_count)
    pieces = []
    for blk_no in range(row_count // block_rows):
        first_row = blk_no * block_rows
        key_end = first_row + block_rows
        query_blk = queries[first_row:key_end]
        query_pos = first_row + jnp.arange(block_rows, dtype=jnp.int32)
        query_seg = seg_float[first_row:key_end]
        scores = jnp.einsum(
            "bhd,shd->hbs", query_blk, key_map[:key_end], preferred_element_type=jnp.float32
        )
        visible = (jnp.arange(key_end, dtype=jnp.int32)[None, :] <= query_pos[:, None]) & (
            seg_float[None, :key_end] == query_seg[:, None]
        )
        weights = jnp.where(visible[None], scores, 0.0).astype(jnp.bfloat16)
        pieces.append(
            jnp.einsum("hbs,she->bhe", weights, values[:key_end], preferred_element_type=jnp.float32)
        )
    local_part = jnp.concatenate(pieces, axis=0)

    state_low = state_in.astype(jnp.bfloat16)
    prefix = jnp.einsum("thd,hde->the", queries, state_low, preferred_element_type=jnp.float32)
    prefix = jnp.where((seg_float == tail_in)[:, None, None], prefix, 0.0)
    numerator = local_part + prefix
    inv_norm = lax.rsqrt(jnp.mean(numerator * numerator, axis=-1, keepdims=True) + 1e-05)
    result = numerator * inv_norm * out_gain.reshape(head_count, HEAD_DIM)
    return result.astype(jnp.bfloat16).reshape(row_count, head_count * HEAD_DIM)


def solution(mesh):
    shape = dict(zip(mesh.axis_names, mesh.devices.shape))
    head = shape["head"]
    fine = Mesh(mesh.devices.reshape(-1, 4, 2, head), (*CTX, "head"))
    placed = (P(CTX, "head"), P(None, CTX, "head"), P("head"), P(CTX))
    return jax.shard_map(
        per_device, mesh=fine, in_specs=placed, out_specs=P(CTX, "head"), check_vma=False
    )
```

```python
import jax
import jax.numpy as jnp
from jax import lax
from jax.sharding import Mesh
from jax.sharding import PartitionSpec as P

HEAD_DIM = 128
SPAN = 16384


CTX = ("y", "x", "core")


def shifted(value, axis, steps, count):
    return lax.ppermute(value, axis, [(source, source + steps) for source in range(count - steps)])


def ring_gather(value, axis, count, dim):
    by_offset = {0: value}
    ahead = value
    behind = value
    for step in range(1, count // 2 + 1):
        ahead = lax.ppermute(ahead, axis, [(j, (j + 1) % count) for j in range(count)])
        by_offset[-step] = ahead
        if step < count - count // 2:
            behind = lax.ppermute(behind, axis, [(j, (j - 1) % count) for j in range(count)])
            by_offset[step] = behind
    low = -(count // 2)
    stacked = jnp.stack([by_offset[off] for off in range(low, low + count)], axis=0)
    ordered = jnp.roll(stacked, lax.axis_index(axis) + low, axis=0)
    moved = jnp.moveaxis(ordered, 0, dim)
    shape = list(value.shape)
    shape[dim] *= count
    return moved.reshape(shape)


def gather_weights(w_local):
    half = w_local.shape[2] // 2
    core = lax.axis_index("core")
    partner = lax.ppermute(w_local, "core", [(0, 1), (1, 0)])
    low_rows = jnp.where(core == 0, w_local[:, :, :half], partner[:, :, half:])
    high_rows = jnp.where(core == 0, partner[:, :, :half], w_local[:, :, half:])
    rows = jnp.concatenate([low_rows, high_rows], axis=1)
    rows = ring_gather(rows, "x", lax.axis_size("x"), 1)
    rows = ring_gather(rows, "y", lax.axis_size("y"), 1)
    other = lax.ppermute(rows, "core", [(0, 1), (1, 0)])
    return jnp.where(
        core == 0,
        jnp.concatenate([rows, other], axis=2),
        jnp.concatenate([other, rows], axis=2),
    )


def feature_map(values):
    return (jax.nn.elu(values.astype(jnp.float32)) + 1.0).astype(jnp.bfloat16)


def state_scan(kv_state, tails, row_count, held):
    count = lax.axis_size(CTX)
    window = min(count - 1, 1 + (SPAN - 1) // row_count)
    row_len = lax.axis_size("x") * lax.axis_size("core")
    assert window <= 2 * row_len
    me = lax.axis_index(CTX)
    pos = me % row_len
    first = me - pos

    def tail_of(block):
        return jnp.where(block >= 0, tails[jnp.clip(block, 0, count - 1)], -1.0)

    prev_tail = tail_of(me - 1)
    spread = jnp.broadcast_to(kv_state.astype(jnp.bfloat16)[None], (row_len,) + kv_state.shape)
    row = lax.all_to_all(spread, ("x", "core"), 0, 0, tiled=True).astype(jnp.float32)
    row, held = lax.optimization_barrier((row, held))
    places = jnp.arange(row_len)
    row_tails = tail_of(first + places)
    in_last = row_tails == row_tails[row_len - 1]

    def masked(mask):
        return jnp.sum(jnp.where(mask[:, None, None, None], row, 0.0), axis=0)

    y_count = lax.axis_size("y")
    one_back = shifted(masked(in_last).astype(jnp.bfloat16), "y", 1, y_count).astype(jnp.float32)
    two_back = shifted(
        masked(in_last & (places >= pos)).astype(jnp.bfloat16), "y", 2, y_count
    ).astype(jnp.float32)
    state = masked((places < pos) & (row_tails == prev_tail))
    state = state + jnp.where(tail_of(first - 1) == prev_tail, one_back, 0.0)
    if window > row_len:
        state = state + jnp.where(tail_of(first - row_len - 1) == prev_tail, two_back, 0.0)
    return state, prev_tail, held


def per_device(tokens, w_qkv, out_gain, seg_ids):
    whole = lax.all_gather(tokens, "head", axis=1, tiled=True)
    row_count = seg_ids.shape[0]
    groups = lax.axis_size(CTX)
    own_rows = w_qkv.shape[1]
    tail_row = jnp.full((w_qkv.shape[0], 1, w_qkv.shape[2]), seg_ids[-1], w_qkv.dtype)
    carried = gather_weights(jnp.concatenate([w_qkv, tail_row], axis=1))
    carried = carried.reshape(w_qkv.shape[0], groups, own_rows + 1, w_qkv.shape[2])
    w_rows = carried[:, :, :own_rows].reshape(w_qkv.shape[0], groups * own_rows, w_qkv.shape[2])
    tails = carried[0, :, own_rows, 0].astype(jnp.float32)
    key_value = jnp.einsum(
        "tr,grc->gtc", whole, w_rows[1:], preferred_element_type=jnp.float32
    ).astype(jnp.bfloat16)
    head_count = key_value.shape[2] // HEAD_DIM
    key_map = feature_map(key_value[0]).reshape(row_count, head_count, HEAD_DIM)
    values = key_value[1].reshape(row_count, head_count, HEAD_DIM)
    seg_float = seg_ids.astype(jnp.float32)
    tail_id = seg_float[-1]
    key_tail = jnp.where((seg_float == tail_id)[:, None, None], key_map, jnp.zeros_like(key_map))
    kv_state = jnp.einsum("thd,the->hde", key_tail, values, preferred_element_type=jnp.float32)

    tails, kv_state = lax.optimization_barrier((tails, kv_state))
    query_proj = jnp.einsum("tr,rc->tc", whole, w_rows[0], preferred_element_type=jnp.float32)
    query_proj = lax.reduce_precision(query_proj, exponent_bits=8, mantissa_bits=7)
    queries = feature_map(query_proj).reshape(row_count, head_count, HEAD_DIM)
    split = min(512, row_count)
    state_in, tail_in, late_queries = state_scan(kv_state, tails, row_count, queries[split:])
    queries_used = jnp.concatenate([queries[:split], late_queries], axis=0)

    block_rows = min(512, row_count)
    pieces = []
    for blk_no in range(row_count // block_rows):
        first_row = blk_no * block_rows
        key_end = first_row + block_rows
        query_blk = queries_used[first_row:key_end]
        query_pos = first_row + jnp.arange(block_rows, dtype=jnp.int32)
        query_seg = seg_float[first_row:key_end]
        scores = jnp.einsum(
            "bhd,shd->hbs", query_blk, key_map[:key_end], preferred_element_type=jnp.float32
        )
        visible = (jnp.arange(key_end, dtype=jnp.int32)[None, :] <= query_pos[:, None]) & (
            seg_float[None, :key_end] == query_seg[:, None]
        )
        weights = jnp.where(visible[None], scores, 0.0).astype(jnp.bfloat16)
        pieces.append(
            jnp.einsum("hbs,she->bhe", weights, values[:key_end], preferred_element_type=jnp.float32)
        )
    local_part = jnp.concatenate(pieces, axis=0)

    state_low = state_in.astype(jnp.bfloat16)
    prefix = jnp.einsum("thd,hde->the", queries, state_low, preferred_element_type=jnp.float32)
    prefix = jnp.where((seg_float == tail_in)[:, None, None], prefix, 0.0)
    numerator = local_part + prefix
    inv_norm = lax.rsqrt(jnp.mean(numerator * numerator, axis=-1, keepdims=True) + 1e-05)
    result = numerator * inv_norm * out_gain.reshape(head_count, HEAD_DIM)
    return result.astype(jnp.bfloat16).reshape(row_count, head_count * HEAD_DIM)


def solution(mesh):
    shape = dict(zip(mesh.axis_names, mesh.devices.shape))
    head = shape["head"]
    fine = Mesh(mesh.devices.reshape(-1, 4, 2, head), (*CTX, "head"))
    placed = (P(CTX, "head"), P(None, CTX, "head"), P("head"), P(CTX))
    return jax.shard_map(
        per_device, mesh=fine, in_specs=placed, out_specs=P(CTX, "head"), check_vma=False
    )
```

```python
import jax
import jax.numpy as jnp
from jax import lax
from jax.sharding import Mesh
from jax.sharding import PartitionSpec as P

HEAD_DIM = 128
SPAN = 16384


CTX = ("y", "x", "core")


def shifted(value, axis, steps, count):
    return lax.ppermute(value, axis, [(source, source + steps) for source in range(count - steps)])


def ring_gather(value, axis, count, dim):
    by_offset = {0: value}
    ahead = value
    behind = value
    for step in range(1, count // 2 + 1):
        ahead = lax.ppermute(ahead, axis, [(j, (j + 1) % count) for j in range(count)])
        by_offset[-step] = ahead
        if step < count - count // 2:
            behind = lax.ppermute(behind, axis, [(j, (j - 1) % count) for j in range(count)])
            by_offset[step] = behind
    low = -(count // 2)
    stacked = jnp.stack([by_offset[off] for off in range(low, low + count)], axis=0)
    ordered = jnp.roll(stacked, lax.axis_index(axis) + low, axis=0)
    moved = jnp.moveaxis(ordered, 0, dim)
    shape = list(value.shape)
    shape[dim] *= count
    return moved.reshape(shape)


def gather_weights(w_local):
    half = w_local.shape[2] // 2
    core = lax.axis_index("core")
    partner = lax.ppermute(w_local, "core", [(0, 1), (1, 0)])
    low_rows = jnp.where(core == 0, w_local[:, :, :half], partner[:, :, half:])
    high_rows = jnp.where(core == 0, partner[:, :, :half], w_local[:, :, half:])
    rows = jnp.concatenate([low_rows, high_rows], axis=1)
    rows = ring_gather(rows, "x", lax.axis_size("x"), 1)
    rows = ring_gather(rows, "y", lax.axis_size("y"), 1)
    other = lax.ppermute(rows, "core", [(0, 1), (1, 0)])
    return jnp.where(
        core == 0,
        jnp.concatenate([rows, other], axis=2),
        jnp.concatenate([other, rows], axis=2),
    )


def feature_map(values):
    return (jax.nn.elu(values.astype(jnp.float32)) + 1.0).astype(jnp.bfloat16)


def state_scan(kv_state, tails, row_count):
    count = lax.axis_size(CTX)
    window = min(count - 1, 1 + (SPAN - 1) // row_count)
    row_len = lax.axis_size("x") * lax.axis_size("core")
    assert window <= 2 * row_len
    me = lax.axis_index(CTX)
    pos = me % row_len
    first = me - pos

    def tail_of(block):
        return jnp.where(block >= 0, tails[jnp.clip(block, 0, count - 1)], -1.0)

    prev_tail = tail_of(me - 1)
    spread = jnp.broadcast_to(kv_state.astype(jnp.bfloat16)[None], (row_len,) + kv_state.shape)
    row = lax.all_to_all(spread, ("x", "core"), 0, 0, tiled=True).astype(jnp.float32)
    places = jnp.arange(row_len)
    row_tails = tail_of(first + places)
    in_last = row_tails == row_tails[row_len - 1]

    def masked(mask):
        return jnp.sum(jnp.where(mask[:, None, None, None], row, 0.0), axis=0)

    y_count = lax.axis_size("y")
    assert y_count > 2
    y = lax.axis_index("y")
    send = jnp.zeros((y_count,) + kv_state.shape, jnp.bfloat16)
    send = send.at[(y + 1) % y_count].set(masked(in_last).astype(jnp.bfloat16))
    send = send.at[(y + 2) % y_count].set(masked(in_last & (places >= pos)).astype(jnp.bfloat16))
    got = lax.all_to_all(send, "y", 0, 0, tiled=True)
    one_back = got[(y + y_count - 1) % y_count].astype(jnp.float32)
    two_back = got[(y + y_count - 2) % y_count].astype(jnp.float32)
    state = masked((places < pos) & (row_tails == prev_tail))
    state = state + jnp.where((y >= 1) & (tail_of(first - 1) == prev_tail), one_back, 0.0)
    if window > row_len:
        state = state + jnp.where(
            (y >= 2) & (tail_of(first - row_len - 1) == prev_tail), two_back, 0.0
        )
    return state, prev_tail


def per_device(tokens, w_qkv, out_gain, seg_ids):
    whole = lax.all_gather(tokens, "head", axis=1, tiled=True)
    row_count = seg_ids.shape[0]
    groups = lax.axis_size(CTX)
    own_rows = w_qkv.shape[1]
    tail_row = jnp.full((w_qkv.shape[0], 1, w_qkv.shape[2]), seg_ids[-1], w_qkv.dtype)
    carried = gather_weights(jnp.concatenate([w_qkv, tail_row], axis=1))
    carried = carried.reshape(w_qkv.shape[0], groups, own_rows + 1, w_qkv.shape[2])
    w_rows = carried[:, :, :own_rows].reshape(w_qkv.shape[0], groups * own_rows, w_qkv.shape[2])
    tails = carried[0, :, own_rows, 0].astype(jnp.float32)
    key_value = jnp.einsum(
        "tr,grc->gtc", whole, w_rows[1:], preferred_element_type=jnp.float32
    ).astype(jnp.bfloat16)
    head_count = key_value.shape[2] // HEAD_DIM
    key_map = feature_map(key_value[0]).reshape(row_count, head_count, HEAD_DIM)
    values = key_value[1].reshape(row_count, head_count, HEAD_DIM)
    seg_float = seg_ids.astype(jnp.float32)
    tail_id = seg_float[-1]
    key_tail = jnp.where((seg_float == tail_id)[:, None, None], key_map, jnp.zeros_like(key_map))
    kv_state = jnp.einsum("thd,the->hde", key_tail, values, preferred_element_type=jnp.float32)

    tails, kv_state = lax.optimization_barrier((tails, kv_state))
    state_in, tail_in = state_scan(kv_state, tails, row_count)
    query_proj = jnp.einsum("tr,rc->tc", whole, w_rows[0], preferred_element_type=jnp.float32)
    query_proj = lax.reduce_precision(query_proj, exponent_bits=8, mantissa_bits=7)
    queries = feature_map(query_proj).reshape(row_count, head_count, HEAD_DIM)

    block_rows = min(512, row_count)
    pieces = []
    for blk_no in range(row_count // block_rows):
        first_row = blk_no * block_rows
        key_end = first_row + block_rows
        query_blk = queries[first_row:key_end]
        query_pos = first_row + jnp.arange(block_rows, dtype=jnp.int32)
        query_seg = seg_float[first_row:key_end]
        scores = jnp.einsum(
            "bhd,shd->hbs", query_blk, key_map[:key_end], preferred_element_type=jnp.float32
        )
        visible = (jnp.arange(key_end, dtype=jnp.int32)[None, :] <= query_pos[:, None]) & (
            seg_float[None, :key_end] == query_seg[:, None]
        )
        weights = jnp.where(visible[None], scores, 0.0).astype(jnp.bfloat16)
        pieces.append(
            jnp.einsum("hbs,she->bhe", weights, values[:key_end], preferred_element_type=jnp.float32)
        )
    local_part = jnp.concatenate(pieces, axis=0)

    state_low = state_in.astype(jnp.bfloat16)
    prefix = jnp.einsum("thd,hde->the", queries, state_low, preferred_element_type=jnp.float32)
    prefix = jnp.where((seg_float == tail_in)[:, None, None], prefix, 0.0)
    numerator = local_part + prefix
    inv_norm = lax.rsqrt(jnp.mean(numerator * numerator, axis=-1, keepdims=True) + 1e-05)
    result = numerator * inv_norm * out_gain.reshape(head_count, HEAD_DIM)
    return result.astype(jnp.bfloat16).reshape(row_count, head_count * HEAD_DIM)


def solution(mesh):
    shape = dict(zip(mesh.axis_names, mesh.devices.shape))
    head = shape["head"]
    fine = Mesh(mesh.devices.reshape(-1, 4, 2, head), (*CTX, "head"))
    placed = (P(CTX, "head"), P(None, CTX, "head"), P("head"), P(CTX))
    return jax.shard_map(
        per_device, mesh=fine, in_specs=placed, out_specs=P(CTX, "head"), check_vma=False
    )
```

```python
import jax
import jax.numpy as jnp
from jax import lax
from jax.sharding import Mesh
from jax.sharding import PartitionSpec as P

HEAD_DIM = 128
SPAN = 16384


CTX = ("y_hi", "y_lo", "x", "core")
Y = ("y_hi", "y_lo")


def shifted(value, axis, steps, count):
    return lax.ppermute(value, axis, [(source, source + steps) for source in range(count - steps)])


def ring_gather(value, axis, count, dim):
    by_offset = {0: value}
    ahead = value
    behind = value
    for step in range(1, count // 2 + 1):
        ahead = lax.ppermute(ahead, axis, [(j, (j + 1) % count) for j in range(count)])
        by_offset[-step] = ahead
        if step < count - count // 2:
            behind = lax.ppermute(behind, axis, [(j, (j - 1) % count) for j in range(count)])
            by_offset[step] = behind
    low = -(count // 2)
    stacked = jnp.stack([by_offset[off] for off in range(low, low + count)], axis=0)
    ordered = jnp.roll(stacked, lax.axis_index(axis) + low, axis=0)
    moved = jnp.moveaxis(ordered, 0, dim)
    shape = list(value.shape)
    shape[dim] *= count
    return moved.reshape(shape)


def gather_weights(w_local):
    half = w_local.shape[2] // 2
    core = lax.axis_index("core")
    partner = lax.ppermute(w_local, "core", [(0, 1), (1, 0)])
    low_rows = jnp.where(core == 0, w_local[:, :, :half], partner[:, :, half:])
    high_rows = jnp.where(core == 0, partner[:, :, :half], w_local[:, :, half:])
    rows = jnp.concatenate([low_rows, high_rows], axis=1)
    rows = ring_gather(rows, "x", lax.axis_size("x"), 1)
    rows = ring_gather(rows, Y, lax.axis_size(Y), 1)
    other = lax.ppermute(rows, "core", [(0, 1), (1, 0)])
    return jnp.where(
        core == 0,
        jnp.concatenate([rows, other], axis=2),
        jnp.concatenate([other, rows], axis=2),
    )


def feature_map(values):
    return (jax.nn.elu(values.astype(jnp.float32)) + 1.0).astype(jnp.bfloat16)


def state_scan(kv_state, tails, row_count):
    count = lax.axis_size(CTX)
    window = min(count - 1, 1 + (SPAN - 1) // row_count)
    group = ("y_lo", "x", "core")
    group_len = lax.axis_size(group)
    assert window <= group_len
    me = lax.axis_index(CTX)
    pos = me % group_len
    first = me - pos

    def tail_of(block):
        return jnp.where(block >= 0, tails[jnp.clip(block, 0, count - 1)], -1.0)

    prev_tail = tail_of(me - 1)
    spread = jnp.broadcast_to(kv_state.astype(jnp.bfloat16)[None], (group_len,) + kv_state.shape)
    block_states = lax.all_to_all(spread, group, 0, 0, tiled=True).astype(jnp.float32)
    places = jnp.arange(group_len)
    group_tails = tail_of(first + places)
    in_last = group_tails == group_tails[group_len - 1]

    def masked(mask):
        return jnp.sum(jnp.where(mask[:, None, None, None], block_states, 0.0), axis=0)

    rest = masked(in_last & (places >= pos)).astype(jnp.bfloat16)
    one_back = shifted(rest, "y_hi", 1, lax.axis_size("y_hi")).astype(jnp.float32)
    state = masked((places < pos) & (group_tails == prev_tail))
    state = state + jnp.where(
        (first > 0) & (tail_of(first - 1) == prev_tail), one_back, 0.0
    )
    return state, prev_tail


def per_device(tokens, w_qkv, out_gain, seg_ids):
    whole = lax.all_gather(tokens, "head", axis=1, tiled=True)
    row_count = seg_ids.shape[0]
    groups = lax.axis_size(CTX)
    own_rows = w_qkv.shape[1]
    tail_row = jnp.full((w_qkv.shape[0], 1, w_qkv.shape[2]), seg_ids[-1], w_qkv.dtype)
    carried = gather_weights(jnp.concatenate([w_qkv, tail_row], axis=1))
    carried = carried.reshape(w_qkv.shape[0], groups, own_rows + 1, w_qkv.shape[2])
    w_rows = carried[:, :, :own_rows].reshape(w_qkv.shape[0], groups * own_rows, w_qkv.shape[2])
    tails = carried[0, :, own_rows, 0].astype(jnp.float32)
    key_value = jnp.einsum(
        "tr,grc->gtc", whole, w_rows[1:], preferred_element_type=jnp.float32
    ).astype(jnp.bfloat16)
    head_count = key_value.shape[2] // HEAD_DIM
    key_map = feature_map(key_value[0]).reshape(row_count, head_count, HEAD_DIM)
    values = key_value[1].reshape(row_count, head_count, HEAD_DIM)
    seg_float = seg_ids.astype(jnp.float32)
    tail_id = seg_float[-1]
    key_tail = jnp.where((seg_float == tail_id)[:, None, None], key_map, jnp.zeros_like(key_map))
    kv_state = jnp.einsum("thd,the->hde", key_tail, values, preferred_element_type=jnp.float32)

    tails, kv_state = lax.optimization_barrier((tails, kv_state))
    state_in, tail_in = state_scan(kv_state, tails, row_count)
    query_proj = jnp.einsum("tr,rc->tc", whole, w_rows[0], preferred_element_type=jnp.float32)
    query_proj = lax.reduce_precision(query_proj, exponent_bits=8, mantissa_bits=7)
    queries = feature_map(query_proj).reshape(row_count, head_count, HEAD_DIM)

    block_rows = min(512, row_count)
    pieces = []
    for blk_no in range(row_count // block_rows):
        first_row = blk_no * block_rows
        key_end = first_row + block_rows
        query_blk = queries[first_row:key_end]
        query_pos = first_row + jnp.arange(block_rows, dtype=jnp.int32)
        query_seg = seg_float[first_row:key_end]
        scores = jnp.einsum(
            "bhd,shd->hbs", query_blk, key_map[:key_end], preferred_element_type=jnp.float32
        )
        visible = (jnp.arange(key_end, dtype=jnp.int32)[None, :] <= query_pos[:, None]) & (
            seg_float[None, :key_end] == query_seg[:, None]
        )
        weights = jnp.where(visible[None], scores, 0.0).astype(jnp.bfloat16)
        pieces.append(
            jnp.einsum("hbs,she->bhe", weights, values[:key_end], preferred_element_type=jnp.float32)
        )
    local_part = jnp.concatenate(pieces, axis=0)

    state_low = state_in.astype(jnp.bfloat16)
    prefix = jnp.einsum("thd,hde->the", queries, state_low, preferred_element_type=jnp.float32)
    prefix = jnp.where((seg_float == tail_in)[:, None, None], prefix, 0.0)
    numerator = local_part + prefix
    inv_norm = lax.rsqrt(jnp.mean(numerator * numerator, axis=-1, keepdims=True) + 1e-05)
    result = numerator * inv_norm * out_gain.reshape(head_count, HEAD_DIM)
    return result.astype(jnp.bfloat16).reshape(row_count, head_count * HEAD_DIM)


def solution(mesh):
    shape = dict(zip(mesh.axis_names, mesh.devices.shape))
    head = shape["head"]
    fine = Mesh(mesh.devices.reshape(-1, 2, 4, 2, head), (*CTX, "head"))
    placed = (P(CTX, "head"), P(None, CTX, "head"), P("head"), P(CTX))
    return jax.shard_map(
        per_device, mesh=fine, in_specs=placed, out_specs=P(CTX, "head"), check_vma=False
    )
```

```python
import jax
import jax.numpy as jnp
from jax import lax
from jax.sharding import Mesh
from jax.sharding import PartitionSpec as P

HEAD_DIM = 128
SPAN = 16384


CTX = ("y", "x", "core")


def shifted(value, axis, steps, count):
    return lax.ppermute(value, axis, [(source, source + steps) for source in range(count - steps)])


def ring_gather(value, axis, count, dim):
    by_offset = {0: value}
    ahead = value
    behind = value
    for step in range(1, count // 2 + 1):
        ahead = lax.ppermute(ahead, axis, [(j, (j + 1) % count) for j in range(count)])
        by_offset[-step] = ahead
        if step < count - count // 2:
            behind = lax.ppermute(behind, axis, [(j, (j - 1) % count) for j in range(count)])
            by_offset[step] = behind
    low = -(count // 2)
    stacked = jnp.stack([by_offset[off] for off in range(low, low + count)], axis=0)
    ordered = jnp.roll(stacked, lax.axis_index(axis) + low, axis=0)
    moved = jnp.moveaxis(ordered, 0, dim)
    shape = list(value.shape)
    shape[dim] *= count
    return moved.reshape(shape)


def gather_weights(w_local):
    half = w_local.shape[2] // 2
    core = lax.axis_index("core")
    partner = lax.ppermute(w_local, "core", [(0, 1), (1, 0)])
    low_rows = jnp.where(core == 0, w_local[:, :, :half], partner[:, :, half:])
    high_rows = jnp.where(core == 0, partner[:, :, :half], w_local[:, :, half:])
    rows = jnp.concatenate([low_rows, high_rows], axis=1)
    rows = direct_gather(rows, "x", lax.axis_size("x"), 1)
    rows = ring_gather(rows, "y", lax.axis_size("y"), 1)
    other = lax.ppermute(rows, "core", [(0, 1), (1, 0)])
    return jnp.where(
        core == 0,
        jnp.concatenate([rows, other], axis=2),
        jnp.concatenate([other, rows], axis=2),
    )


def direct_gather(value, axis, count, dim):
    low = -(count // 2)
    by_offset = {0: value}
    for off in range(low, low + count):
        if off != 0:
            by_offset[off] = lax.ppermute(value, axis, [(j, (j - off) % count) for j in range(count)])
    stacked = jnp.stack([by_offset[off] for off in range(low, low + count)], axis=0)
    ordered = jnp.roll(stacked, lax.axis_index(axis) + low, axis=0)
    moved = jnp.moveaxis(ordered, 0, dim)
    shape = list(value.shape)
    shape[dim] *= count
    return moved.reshape(shape)


def feature_map(values):
    return (jax.nn.elu(values.astype(jnp.float32)) + 1.0).astype(jnp.bfloat16)


def state_scan(kv_state, tails, row_count):
    count = lax.axis_size(CTX)
    window = min(count - 1, 1 + (SPAN - 1) // row_count)
    row_len = lax.axis_size("x") * lax.axis_size("core")
    assert window <= 2 * row_len
    me = lax.axis_index(CTX)
    pos = me % row_len
    first = me - pos

    def tail_of(block):
        return jnp.where(block >= 0, tails[jnp.clip(block, 0, count - 1)], -1.0)

    prev_tail = tail_of(me - 1)
    spread = jnp.broadcast_to(kv_state.astype(jnp.bfloat16)[None], (row_len,) + kv_state.shape)
    row = lax.all_to_all(spread, ("x", "core"), 0, 0, tiled=True).astype(jnp.float32)
    places = jnp.arange(row_len)
    row_tails = tail_of(first + places)
    in_last = row_tails == row_tails[row_len - 1]

    def masked(mask):
        return jnp.sum(jnp.where(mask[:, None, None, None], row, 0.0), axis=0)

    y_count = lax.axis_size("y")
    one_back = shifted(masked(in_last).astype(jnp.bfloat16), "y", 1, y_count).astype(jnp.float32)
    two_back = shifted(
        masked(in_last & (places >= pos)).astype(jnp.bfloat16), "y", 2, y_count
    ).astype(jnp.float32)
    state = masked((places < pos) & (row_tails == prev_tail))
    state = state + jnp.where(tail_of(first - 1) == prev_tail, one_back, 0.0)
    if window > row_len:
        state = state + jnp.where(tail_of(first - row_len - 1) == prev_tail, two_back, 0.0)
    return state, prev_tail


def per_device(tokens, w_qkv, out_gain, seg_ids):
    whole = lax.all_gather(tokens, "head", axis=1, tiled=True)
    row_count = seg_ids.shape[0]
    groups = lax.axis_size(CTX)
    own_rows = w_qkv.shape[1]
    tail_row = jnp.full((w_qkv.shape[0], 1, w_qkv.shape[2]), seg_ids[-1], w_qkv.dtype)
    carried = gather_weights(jnp.concatenate([w_qkv, tail_row], axis=1))
    carried = carried.reshape(w_qkv.shape[0], groups, own_rows + 1, w_qkv.shape[2])
    w_rows = carried[:, :, :own_rows].reshape(w_qkv.shape[0], groups * own_rows, w_qkv.shape[2])
    tails = carried[0, :, own_rows, 0].astype(jnp.float32)
    key_value = jnp.einsum(
        "tr,grc->gtc", whole, w_rows[1:], preferred_element_type=jnp.float32
    ).astype(jnp.bfloat16)
    head_count = key_value.shape[2] // HEAD_DIM
    key_map = feature_map(key_value[0]).reshape(row_count, head_count, HEAD_DIM)
    values = key_value[1].reshape(row_count, head_count, HEAD_DIM)
    seg_float = seg_ids.astype(jnp.float32)
    tail_id = seg_float[-1]
    key_tail = jnp.where((seg_float == tail_id)[:, None, None], key_map, jnp.zeros_like(key_map))
    kv_state = jnp.einsum("thd,the->hde", key_tail, values, preferred_element_type=jnp.float32)

    tails, kv_state = lax.optimization_barrier((tails, kv_state))
    state_in, tail_in = state_scan(kv_state, tails, row_count)
    query_proj = jnp.einsum("tr,rc->tc", whole, w_rows[0], preferred_element_type=jnp.float32)
    query_proj = lax.reduce_precision(query_proj, exponent_bits=8, mantissa_bits=7)
    queries = feature_map(query_proj).reshape(row_count, head_count, HEAD_DIM)

    block_rows = min(512, row_count)
    pieces = []
    for blk_no in range(row_count // block_rows):
        first_row = blk_no * block_rows
        key_end = first_row + block_rows
        query_blk = queries[first_row:key_end]
        query_pos = first_row + jnp.arange(block_rows, dtype=jnp.int32)
        query_seg = seg_float[first_row:key_end]
        scores = jnp.einsum(
            "bhd,shd->hbs", query_blk, key_map[:key_end], preferred_element_type=jnp.float32
        )
        visible = (jnp.arange(key_end, dtype=jnp.int32)[None, :] <= query_pos[:, None]) & (
            seg_float[None, :key_end] == query_seg[:, None]
        )
        weights = jnp.where(visible[None], scores, 0.0).astype(jnp.bfloat16)
        pieces.append(
            jnp.einsum("hbs,she->bhe", weights, values[:key_end], preferred_element_type=jnp.float32)
        )
    local_part = jnp.concatenate(pieces, axis=0)

    state_low = state_in.astype(jnp.bfloat16)
    prefix = jnp.einsum("thd,hde->the", queries, state_low, preferred_element_type=jnp.float32)
    prefix = jnp.where((seg_float == tail_in)[:, None, None], prefix, 0.0)
    numerator = local_part + prefix
    inv_norm = lax.rsqrt(jnp.mean(numerator * numerator, axis=-1, keepdims=True) + 1e-05)
    result = numerator * inv_norm * out_gain.reshape(head_count, HEAD_DIM)
    return result.astype(jnp.bfloat16).reshape(row_count, head_count * HEAD_DIM)


def solution(mesh):
    shape = dict(zip(mesh.axis_names, mesh.devices.shape))
    head = shape["head"]
    fine = Mesh(mesh.devices.reshape(-1, 4, 2, head), (*CTX, "head"))
    placed = (P(CTX, "head"), P(None, CTX, "head"), P("head"), P(CTX))
    return jax.shard_map(
        per_device, mesh=fine, in_specs=placed, out_specs=P(CTX, "head"), check_vma=False
    )
```

```python
import jax
import jax.numpy as jnp
from jax import lax
from jax.sharding import Mesh
from jax.sharding import PartitionSpec as P

HEAD_DIM = 128
SPAN = 16384


CTX = ("y", "x", "core")


def shifted(value, axis, steps, count):
    return lax.ppermute(value, axis, [(source, source + steps) for source in range(count - steps)])


def ring_gather(value, axis, count, dim):
    by_offset = {0: value}
    ahead = value
    behind = value
    for step in range(1, count // 2 + 1):
        ahead = lax.ppermute(ahead, axis, [(j, (j + 1) % count) for j in range(count)])
        by_offset[-step] = ahead
        if step < count - count // 2:
            behind = lax.ppermute(behind, axis, [(j, (j - 1) % count) for j in range(count)])
            by_offset[step] = behind
    low = -(count // 2)
    stacked = jnp.stack([by_offset[off] for off in range(low, low + count)], axis=0)
    ordered = jnp.roll(stacked, lax.axis_index(axis) + low, axis=0)
    moved = jnp.moveaxis(ordered, 0, dim)
    shape = list(value.shape)
    shape[dim] *= count
    return moved.reshape(shape)


def gather_weights(w_local):
    half = w_local.shape[2] // 2
    core = lax.axis_index("core")
    x_count = lax.axis_size("x")
    gathered = direct_gather(w_local, "x", x_count, 1)
    partner = lax.ppermute(gathered, "core", [(0, 1), (1, 0)])
    own_half = jnp.where(core == 0, gathered[:, :, :half], gathered[:, :, half:])
    partner_half = jnp.where(core == 0, partner[:, :, :half], partner[:, :, half:])
    core0_rows = jnp.where(core == 0, own_half, partner_half)
    core1_rows = jnp.where(core == 0, partner_half, own_half)
    groups, per = w_local.shape[0], w_local.shape[1]
    rows = jnp.stack(
        [core0_rows.reshape(groups, x_count, per, half), core1_rows.reshape(groups, x_count, per, half)],
        axis=2,
    ).reshape(groups, x_count * 2 * per, half)
    rows = ring_gather(rows, "y", lax.axis_size("y"), 1)
    other = lax.ppermute(rows, "core", [(0, 1), (1, 0)])
    return jnp.where(
        core == 0,
        jnp.concatenate([rows, other], axis=2),
        jnp.concatenate([other, rows], axis=2),
    )


def direct_gather(value, axis, count, dim):
    low = -(count // 2)
    by_offset = {0: value}
    for off in range(low, low + count):
        if off != 0:
            by_offset[off] = lax.ppermute(value, axis, [(j, (j - off) % count) for j in range(count)])
    stacked = jnp.stack([by_offset[off] for off in range(low, low + count)], axis=0)
    ordered = jnp.roll(stacked, lax.axis_index(axis) + low, axis=0)
    moved = jnp.moveaxis(ordered, 0, dim)
    shape = list(value.shape)
    shape[dim] *= count
    return moved.reshape(shape)


def feature_map(values):
    return (jax.nn.elu(values.astype(jnp.float32)) + 1.0).astype(jnp.bfloat16)


def state_scan(kv_state, tails, row_count):
    count = lax.axis_size(CTX)
    window = min(count - 1, 1 + (SPAN - 1) // row_count)
    row_len = lax.axis_size("x") * lax.axis_size("core")
    assert window <= 2 * row_len
    me = lax.axis_index(CTX)
    pos = me % row_len
    first = me - pos

    def tail_of(block):
        return jnp.where(block >= 0, tails[jnp.clip(block, 0, count - 1)], -1.0)

    prev_tail = tail_of(me - 1)
    spread = jnp.broadcast_to(kv_state.astype(jnp.bfloat16)[None], (row_len,) + kv_state.shape)
    row = lax.all_to_all(spread, ("x", "core"), 0, 0, tiled=True).astype(jnp.float32)
    places = jnp.arange(row_len)
    row_tails = tail_of(first + places)
    in_last = row_tails == row_tails[row_len - 1]

    def masked(mask):
        return jnp.sum(jnp.where(mask[:, None, None, None], row, 0.0), axis=0)

    y_count = lax.axis_size("y")
    one_back = shifted(masked(in_last).astype(jnp.bfloat16), "y", 1, y_count).astype(jnp.float32)
    two_back = shifted(
        masked(in_last & (places >= pos)).astype(jnp.bfloat16), "y", 2, y_count
    ).astype(jnp.float32)
    state = masked((places < pos) & (row_tails == prev_tail))
    state = state + jnp.where(tail_of(first - 1) == prev_tail, one_back, 0.0)
    if window > row_len:
        state = state + jnp.where(tail_of(first - row_len - 1) == prev_tail, two_back, 0.0)
    return state, prev_tail


def per_device(tokens, w_qkv, out_gain, seg_ids):
    whole = lax.all_gather(tokens, "head", axis=1, tiled=True)
    row_count = seg_ids.shape[0]
    groups = lax.axis_size(CTX)
    own_rows = w_qkv.shape[1]
    tail_row = jnp.full((w_qkv.shape[0], 1, w_qkv.shape[2]), seg_ids[-1], w_qkv.dtype)
    carried = gather_weights(jnp.concatenate([w_qkv, tail_row], axis=1))
    carried = carried.reshape(w_qkv.shape[0], groups, own_rows + 1, w_qkv.shape[2])
    w_rows = carried[:, :, :own_rows].reshape(w_qkv.shape[0], groups * own_rows, w_qkv.shape[2])
    tails = carried[0, :, own_rows, 0].astype(jnp.float32)
    key_value = jnp.einsum(
        "tr,grc->gtc", whole, w_rows[1:], preferred_element_type=jnp.float32
    ).astype(jnp.bfloat16)
    head_count = key_value.shape[2] // HEAD_DIM
    key_map = feature_map(key_value[0]).reshape(row_count, head_count, HEAD_DIM)
    values = key_value[1].reshape(row_count, head_count, HEAD_DIM)
    seg_float = seg_ids.astype(jnp.float32)
    tail_id = seg_float[-1]
    key_tail = jnp.where((seg_float == tail_id)[:, None, None], key_map, jnp.zeros_like(key_map))
    kv_state = jnp.einsum("thd,the->hde", key_tail, values, preferred_element_type=jnp.float32)

    tails, kv_state = lax.optimization_barrier((tails, kv_state))
    state_in, tail_in = state_scan(kv_state, tails, row_count)
    query_proj = jnp.einsum("tr,rc->tc", whole, w_rows[0], preferred_element_type=jnp.float32)
    query_proj = lax.reduce_precision(query_proj, exponent_bits=8, mantissa_bits=7)
    queries = feature_map(query_proj).reshape(row_count, head_count, HEAD_DIM)

    block_rows = min(512, row_count)
    pieces = []
    for blk_no in range(row_count // block_rows):
        first_row = blk_no * block_rows
        key_end = first_row + block_rows
        query_blk = queries[first_row:key_end]
        query_pos = first_row + jnp.arange(block_rows, dtype=jnp.int32)
        query_seg = seg_float[first_row:key_end]
        scores = jnp.einsum(
            "bhd,shd->hbs", query_blk, key_map[:key_end], preferred_element_type=jnp.float32
        )
        visible = (jnp.arange(key_end, dtype=jnp.int32)[None, :] <= query_pos[:, None]) & (
            seg_float[None, :key_end] == query_seg[:, None]
        )
        weights = jnp.where(visible[None], scores, 0.0).astype(jnp.bfloat16)
        pieces.append(
            jnp.einsum("hbs,she->bhe", weights, values[:key_end], preferred_element_type=jnp.float32)
        )
    local_part = jnp.concatenate(pieces, axis=0)

    state_low = state_in.astype(jnp.bfloat16)
    prefix = jnp.einsum("thd,hde->the", queries, state_low, preferred_element_type=jnp.float32)
    prefix = jnp.where((seg_float == tail_in)[:, None, None], prefix, 0.0)
    numerator = local_part + prefix
    inv_norm = lax.rsqrt(jnp.mean(numerator * numerator, axis=-1, keepdims=True) + 1e-05)
    result = numerator * inv_norm * out_gain.reshape(head_count, HEAD_DIM)
    return result.astype(jnp.bfloat16).reshape(row_count, head_count * HEAD_DIM)


def solution(mesh):
    shape = dict(zip(mesh.axis_names, mesh.devices.shape))
    head = shape["head"]
    fine = Mesh(mesh.devices.reshape(-1, 4, 2, head), (*CTX, "head"))
    placed = (P(CTX, "head"), P(None, CTX, "head"), P("head"), P(CTX))
    return jax.shard_map(
        per_device, mesh=fine, in_specs=placed, out_specs=P(CTX, "head"), check_vma=False
    )
```

```python
import jax
import jax.numpy as jnp
from jax import lax
from jax.sharding import Mesh
from jax.sharding import PartitionSpec as P

HEAD_DIM = 128
SPAN = 16384


CTX = ("y", "x", "core")


def shifted(value, axis, steps, count):
    return lax.ppermute(value, axis, [(source, source + steps) for source in range(count - steps)])


def ring_gather(value, axis, count, dim):
    by_offset = {0: value}
    ahead = value
    behind = value
    for step in range(1, count // 2 + 1):
        ahead = lax.ppermute(ahead, axis, [(j, (j + 1) % count) for j in range(count)])
        by_offset[-step] = ahead
        if step < count - count // 2:
            behind = lax.ppermute(behind, axis, [(j, (j - 1) % count) for j in range(count)])
            by_offset[step] = behind
    low = -(count // 2)
    stacked = jnp.stack([by_offset[off] for off in range(low, low + count)], axis=0)
    ordered = jnp.roll(stacked, lax.axis_index(axis) + low, axis=0)
    moved = jnp.moveaxis(ordered, 0, dim)
    shape = list(value.shape)
    shape[dim] *= count
    return moved.reshape(shape)


def gather_weights(w_local):
    half = w_local.shape[2] // 2
    core = lax.axis_index("core")
    partner = lax.ppermute(w_local, "core", [(0, 1), (1, 0)])
    low_rows = jnp.where(core == 0, w_local[:, :, :half], partner[:, :, half:])
    high_rows = jnp.where(core == 0, partner[:, :, :half], w_local[:, :, half:])
    rows = jnp.concatenate([low_rows, high_rows], axis=1)
    rows = direct_gather(rows, "x", lax.axis_size("x"), 1)
    rows = direct_gather(rows, "y", lax.axis_size("y"), 1)
    other = lax.ppermute(rows, "core", [(0, 1), (1, 0)])
    return jnp.where(
        core == 0,
        jnp.concatenate([rows, other], axis=2),
        jnp.concatenate([other, rows], axis=2),
    )


def direct_gather(value, axis, count, dim):
    low = -(count // 2)
    by_offset = {0: value}
    for off in range(low, low + count):
        if off != 0:
            by_offset[off] = lax.ppermute(value, axis, [(j, (j - off) % count) for j in range(count)])
    stacked = jnp.stack([by_offset[off] for off in range(low, low + count)], axis=0)
    ordered = jnp.roll(stacked, lax.axis_index(axis) + low, axis=0)
    moved = jnp.moveaxis(ordered, 0, dim)
    shape = list(value.shape)
    shape[dim] *= count
    return moved.reshape(shape)


def feature_map(values):
    return (jax.nn.elu(values.astype(jnp.float32)) + 1.0).astype(jnp.bfloat16)


def state_scan(kv_state, tails, row_count):
    count = lax.axis_size(CTX)
    window = min(count - 1, 1 + (SPAN - 1) // row_count)
    row_len = lax.axis_size("x") * lax.axis_size("core")
    assert window <= 2 * row_len
    me = lax.axis_index(CTX)
    pos = me % row_len
    first = me - pos

    def tail_of(block):
        return jnp.where(block >= 0, tails[jnp.clip(block, 0, count - 1)], -1.0)

    prev_tail = tail_of(me - 1)
    spread = jnp.broadcast_to(kv_state.astype(jnp.bfloat16)[None], (row_len,) + kv_state.shape)
    row = lax.all_to_all(spread, ("x", "core"), 0, 0, tiled=True).astype(jnp.float32)
    places = jnp.arange(row_len)
    row_tails = tail_of(first + places)
    in_last = row_tails == row_tails[row_len - 1]

    def masked(mask):
        return jnp.sum(jnp.where(mask[:, None, None, None], row, 0.0), axis=0)

    y_count = lax.axis_size("y")
    one_back = shifted(masked(in_last).astype(jnp.bfloat16), "y", 1, y_count).astype(jnp.float32)
    two_back = shifted(
        masked(in_last & (places >= pos)).astype(jnp.bfloat16), "y", 2, y_count
    ).astype(jnp.float32)
    state = masked((places < pos) & (row_tails == prev_tail))
    state = state + jnp.where(tail_of(first - 1) == prev_tail, one_back, 0.0)
    if window > row_len:
        state = state + jnp.where(tail_of(first - row_len - 1) == prev_tail, two_back, 0.0)
    return state, prev_tail


def per_device(tokens, w_qkv, out_gain, seg_ids):
    whole = lax.all_gather(tokens, "head", axis=1, tiled=True)
    row_count = seg_ids.shape[0]
    groups = lax.axis_size(CTX)
    own_rows = w_qkv.shape[1]
    tail_row = jnp.full((w_qkv.shape[0], 1, w_qkv.shape[2]), seg_ids[-1], w_qkv.dtype)
    carried = gather_weights(jnp.concatenate([w_qkv, tail_row], axis=1))
    carried = carried.reshape(w_qkv.shape[0], groups, own_rows + 1, w_qkv.shape[2])
    w_rows = carried[:, :, :own_rows].reshape(w_qkv.shape[0], groups * own_rows, w_qkv.shape[2])
    tails = carried[0, :, own_rows, 0].astype(jnp.float32)
    key_value = jnp.einsum(
        "tr,grc->gtc", whole, w_rows[1:], preferred_element_type=jnp.float32
    ).astype(jnp.bfloat16)
    head_count = key_value.shape[2] // HEAD_DIM
    key_map = feature_map(key_value[0]).reshape(row_count, head_count, HEAD_DIM)
    values = key_value[1].reshape(row_count, head_count, HEAD_DIM)
    seg_float = seg_ids.astype(jnp.float32)
    tail_id = seg_float[-1]
    key_tail = jnp.where((seg_float == tail_id)[:, None, None], key_map, jnp.zeros_like(key_map))
    kv_state = jnp.einsum("thd,the->hde", key_tail, values, preferred_element_type=jnp.float32)

    tails, kv_state = lax.optimization_barrier((tails, kv_state))
    state_in, tail_in = state_scan(kv_state, tails, row_count)
    query_proj = jnp.einsum("tr,rc->tc", whole, w_rows[0], preferred_element_type=jnp.float32)
    query_proj = lax.reduce_precision(query_proj, exponent_bits=8, mantissa_bits=7)
    queries = feature_map(query_proj).reshape(row_count, head_count, HEAD_DIM)

    block_rows = min(512, row_count)
    pieces = []
    for blk_no in range(row_count // block_rows):
        first_row = blk_no * block_rows
        key_end = first_row + block_rows
        query_blk = queries[first_row:key_end]
        query_pos = first_row + jnp.arange(block_rows, dtype=jnp.int32)
        query_seg = seg_float[first_row:key_end]
        scores = jnp.einsum(
            "bhd,shd->hbs", query_blk, key_map[:key_end], preferred_element_type=jnp.float32
        )
        visible = (jnp.arange(key_end, dtype=jnp.int32)[None, :] <= query_pos[:, None]) & (
            seg_float[None, :key_end] == query_seg[:, None]
        )
        weights = jnp.where(visible[None], scores, 0.0).astype(jnp.bfloat16)
        pieces.append(
            jnp.einsum("hbs,she->bhe", weights, values[:key_end], preferred_element_type=jnp.float32)
        )
    local_part = jnp.concatenate(pieces, axis=0)

    state_low = state_in.astype(jnp.bfloat16)
    prefix = jnp.einsum("thd,hde->the", queries, state_low, preferred_element_type=jnp.float32)
    prefix = jnp.where((seg_float == tail_in)[:, None, None], prefix, 0.0)
    numerator = local_part + prefix
    inv_norm = lax.rsqrt(jnp.mean(numerator * numerator, axis=-1, keepdims=True) + 1e-05)
    result = numerator * inv_norm * out_gain.reshape(head_count, HEAD_DIM)
    return result.astype(jnp.bfloat16).reshape(row_count, head_count * HEAD_DIM)


def solution(mesh):
    shape = dict(zip(mesh.axis_names, mesh.devices.shape))
    head = shape["head"]
    fine = Mesh(mesh.devices.reshape(-1, 4, 2, head), (*CTX, "head"))
    placed = (P(CTX, "head"), P(None, CTX, "head"), P("head"), P(CTX))
    return jax.shard_map(
        per_device, mesh=fine, in_specs=placed, out_specs=P(CTX, "head"), check_vma=False
    )
```
